32 devices in a mesh: seq: 16 (over z, y, x), head: 2 (over core).
Axes of the slice: x: 2, y: 2, z: 4, core: 2. Of those that a mesh axis runs over, the one named last changes fastest.
Arguments:
- inputs: bfloat16 [4096, 5120], P('seq', 'head'), may hold values from -0.059814453 to 0.059814453
- log_decay: float32 [4096, 80], P('seq', 'head'), may hold values from -0.6 to 0, as said below
- b_proj: bfloat16 [4096, 128], P('seq'), may hold values from -1.796875 to 1.796875
- c_proj: bfloat16 [4096, 128], P('seq'), may hold values from -1.796875 to 1.796875
- grad_out: bfloat16 [4096, 5120], P('seq', 'head'), may hold values from -0.059814453 to 0.059814453
Outputs:
- outputs: bfloat16 [4096, 5120], P('seq', 'head')
- grad_inputs: bfloat16 [4096, 5120], P('seq', 'head')
- grad_log_decay: float32 [4096, 80], P('seq', 'head')
- grad_b: float32 [4096, 128], P('seq')
- grad_c: float32 [4096, 128], P('seq')
The draws below stay inside these ranges and needn't reach their ends.
Inputs may be any that keep to these rules, and one draw needn't show every extreme that they name: log_decay is never positive.
All inputs are finite; a program needn't handle non-finite values.
Results may differ from the reference program's by a relative error of at most 0.01.
Values sent between devices are 32-bit elements; how exact they have to be, the bound alone decides.
No kernel may reach another device: no remote copies, remote signals or barrier semaphores. Data moves between devices by JAX's collectives and lax.ppermute only.
A program may use at most 128 MiB of HBM per device.

```python
import math
from functools import partial
import jax
import jax.numpy as jnp
from jax import lax

ATTENDER_COUNT = 80
HEADDIM = 64
STATE = 128
BLOCK = 256
POSITION_TALLY = 4096


def draw_log_decay(key, part):
    generator_seeds = jax.random.split(key, 6)
    slow_share = 5
    slow_heads = jax.random.randint(generator_seeds[0], (ATTENDER_COUNT,), 0, 10) < slow_share
    slow_rate = jax.random.uniform(generator_seeds[1], (ATTENDER_COUNT,), jnp.float32, 0.2, 0.8) / POSITION_TALLY
    fast_rate = jnp.exp(jax.random.uniform(generator_seeds[2], (ATTENDER_COUNT,), jnp.float32, math.log(1.0 / 400.0), math.log(1.0 / 30.0)))
    forgetting_factors = jnp.where(slow_heads, slow_rate, fast_rate)
    rough_approximation = jnp.exp(jax.random.uniform(generator_seeds[3], (POSITION_TALLY, ATTENDER_COUNT), jnp.float32, math.log(0.5), math.log(2.0)))
    input_sequences = jax.random.randint(generator_seeds[4], (POSITION_TALLY, ATTENDER_COUNT), 0, POSITION_TALLY) < 3
    objective_levels = jax.random.uniform(generator_seeds[5], (POSITION_TALLY, ATTENDER_COUNT), jnp.float32, 0.22, 0.51)
    return -(forgetting_factors[None, :] * rough_approximation) - jnp.where(input_sequences, objective_levels, 0.0)


def steps_of(own_key, shape, cuts, smallest, largest):
    def one(position, blocks):
        draws = jax.random.uniform(jax.random.fold_in(jax.random.fold_in(own_key, 6), position), (blocks,), jnp.float32, smallest / len(cuts), largest / len(cuts))
        return jnp.repeat(jnp.exp(draws), shape[position] // blocks).reshape((-1,) + (1,) * (len(shape) - position - 1))

    level = one(*cuts[0])
    for cut in cuts[1:]:
        level = level * one(*cut)
    return level


def centred(rng, shape, scale, limit, cuts=(), held_as=jnp.bfloat16):
    level = steps_of(rng, shape, cuts, -0.22, 0.18) if cuts else 1.0
    values = jax.random.normal(rng, shape, jnp.float32) * scale * level
    return jnp.minimum(jnp.maximum(values, -limit), limit).astype(held_as)


def setup_inputs(seed: int = 0) -> dict:
    keys = jax.random.split(jax.random.key(seed), 6)
    return {
        "inputs": centred(keys[0], (POSITION_TALLY, ATTENDER_COUNT * HEADDIM), 0.01, 0.059814453, ((0, 16), (1, 2))),
        "log_decay": draw_log_decay(jax.random.fold_in(keys[5], 71), 0),
        "b_proj": centred(keys[2], (POSITION_TALLY, STATE), 0.3, 1.796875, ((0, 16),)),
        "c_proj": centred(keys[3], (POSITION_TALLY, STATE), 0.3, 1.796875, ((0, 16),)),
        "grad_out": centred(keys[4], (POSITION_TALLY, ATTENDER_COUNT * HEADDIM), 0.01, 0.059814453, ((0, 16), (1, 2))),
    }


HIGHEST_PRECISION = lax.Precision.HIGHEST

def to_half(values):
    return lax.optimization_barrier(values.astype(jnp.bfloat16)).astype(jnp.float32)

def block_terms(head_signal, head_decay, b_blocks, scores):
    window = head_decay.shape[1]
    causal = jnp.tril(jnp.ones((window, window), dtype=bool))
    prefix = jnp.cumsum(head_decay, axis=1)
    spread = prefix[:, :, None] - prefix[:, None, :]
    decay_mat = jnp.where(causal, jnp.exp(jnp.where(causal, spread, 0.0)), 0.0)
    weighted = to_half(scores * decay_mat)
    within = jnp.einsum('kts,ksp->ktp', weighted, to_half(head_signal), precision=HIGHEST_PRECISION)
    weights = jnp.exp(prefix[:, -1:] - prefix)
    scaled = to_half(head_signal * weights[:, :, None])
    states = jnp.einsum('ksp,ksn->kpn', scaled, to_half(b_blocks), precision=HIGHEST_PRECISION)
    return (prefix, within, states, prefix[:, -1])

def head_terms(pieces, b_blocks, c_blocks, scores):
    head_signal, head_decay = pieces
    prefix, within, states, totals = block_terms(head_signal, head_decay, b_blocks, scores)

    def advance(running, block_pieces):
        block_total, block_state = block_pieces
        return (jnp.exp(block_total) * running + block_state, running)
    final_state, starts = lax.scan(advance, jnp.zeros(states.shape[1:], jnp.float32), (totals, states))
    carried = jnp.einsum('ktn,kpn->ktp', c_blocks, starts, precision=HIGHEST_PRECISION)
    return within + jnp.exp(prefix)[:, :, None] * carried

def score_blocks(b_proj, c_proj):
    blocks = b_proj.shape[0] // BLOCK
    b_half = b_proj.reshape(blocks, BLOCK, STATE)
    c_half = c_proj.reshape(blocks, BLOCK, STATE)
    return jnp.einsum('ktn,ksn->kts', c_half, b_half, preferred_element_type=jnp.float32)

def whole_terms(signal, decays, b_rows, c_rows, scores):
    tokens, head_count = decays.shape
    blocks = tokens // BLOCK
    head_signal = signal.reshape(blocks, BLOCK, head_count, HEADDIM).transpose(2, 0, 1, 3)
    head_decay = decays.reshape(blocks, BLOCK, head_count).transpose(2, 0, 1)
    b_blocks = b_rows.reshape(blocks, BLOCK, STATE)
    c_blocks = c_rows.reshape(blocks, BLOCK, STATE)
    per_head = jax.checkpoint(partial(head_terms, b_blocks=b_blocks, c_blocks=c_blocks, scores=scores))
    outs_heads = lax.map(per_head, (head_signal, head_decay))
    return outs_heads.transpose(1, 2, 0, 3).reshape(tokens, head_count * HEADDIM)

def reference(inputs, log_decay, b_proj, c_proj, grad_out):
    signal = inputs.astype(jnp.float32)
    b_rows = b_proj.astype(jnp.float32)
    c_rows = c_proj.astype(jnp.float32)
    scores = score_blocks(b_proj, c_proj)
    out_f, pull_back = jax.vjp(whole_terms, signal, log_decay, b_rows, c_rows, scores)
    grad_signal, grad_decay, grad_b, grad_c, grad_scores = pull_back(grad_out.astype(jnp.float32))
    blocks = b_rows.shape[0] // BLOCK
    b_blocks = b_rows.reshape(blocks, BLOCK, STATE)
    c_blocks = c_rows.reshape(blocks, BLOCK, STATE)
    half_scores = to_half(grad_scores)
    grad_c = grad_c + jnp.einsum('kts,ksn->ktn', half_scores, b_blocks, precision=HIGHEST_PRECISION).reshape(-1, STATE)
    grad_b = grad_b + jnp.einsum('kts,ktn->ksn', half_scores, c_blocks, precision=HIGHEST_PRECISION).reshape(-1, STATE)
    return (out_f.astype(jnp.bfloat16), grad_signal.astype(jnp.bfloat16), grad_decay, grad_b, grad_c)
```

```python
import jax
import jax.numpy as jnp
from jax import lax
from jax.sharding import PartitionSpec as P

HEADDIM = 64
STATE = 128
BLOCK = 256

F32 = jnp.float32
BF16 = jnp.bfloat16
HIGHEST = lax.Precision.HIGHEST


def rounded(values):
    return values.astype(BF16).astype(F32)


def combine(early, late):
    early_log, early_state = early
    late_log, late_state = late
    return (early_log + late_log, jnp.exp(late_log) * early_state + late_state)


def cross_device(final, state_grad, total, count):
    heads, width, state = final.shape
    rows = heads * width
    if count == 1:
        zero = jnp.zeros_like(final)
        return zero, zero
    share = rows // count
    payload = jnp.stack(
        [final.reshape(rows, state), state_grad.reshape(rows, state)], axis=1
    )
    got = lax.all_to_all(payload, "seq", 0, 0, tiled=True).reshape(count, share, 2, state)
    totals = lax.all_gather(total, "seq")
    place = lax.axis_index("seq")
    row_heads = (place * share + jnp.arange(share)) // width
    logs = jnp.take(totals, row_heads, axis=1)[:, :, None]
    logs = jnp.broadcast_to(logs, (count, share, 1))
    _, ahead = lax.associative_scan(combine, (logs, got[:, :, 0]))
    _, behind = lax.associative_scan(combine, (logs, got[:, :, 1]), reverse=True)
    zero = jnp.zeros((1, share, state), F32)
    incoming = jnp.concatenate([zero, ahead[:-1]], axis=0)
    adjoint = jnp.concatenate([behind[1:], zero], axis=0)
    back = jnp.stack([incoming, adjoint], axis=2).reshape(count * share, 2, state)
    back = lax.all_to_all(back, "seq", 0, 0, tiled=True)
    return (back[:, 0].reshape(heads, width, state), back[:, 1].reshape(heads, width, state))


def shards(inputs, log_decay, b_proj, c_proj, grad_out, count):
    tokens, head_count = log_decay.shape
    blocks = tokens // BLOCK
    x16 = inputs.reshape(blocks, BLOCK, head_count, HEADDIM).transpose(2, 0, 1, 3)
    g16 = grad_out.reshape(blocks, BLOCK, head_count, HEADDIM).transpose(2, 0, 1, 3)
    xf = x16.astype(F32)
    gf = g16.astype(F32)
    decay = log_decay.reshape(blocks, BLOCK, head_count).transpose(2, 0, 1)
    b16 = b_proj.reshape(blocks, BLOCK, STATE)
    c16 = c_proj.reshape(blocks, BLOCK, STATE)
    bf = b16.astype(F32)
    cf = c16.astype(F32)

    prefix = jnp.cumsum(decay, axis=-1)
    totals = prefix[..., -1]
    causal = jnp.tril(jnp.ones((BLOCK, BLOCK), dtype=bool))
    scores = jnp.einsum("ktn,ksn->kts", c16, b16, preferred_element_type=F32)
    spread = prefix[..., :, None] - prefix[..., None, :]
    decay_mat = jnp.where(causal, jnp.exp(jnp.where(causal, spread, 0.0)), 0.0)
    weighted_f = scores[None] * decay_mat
    weighted = weighted_f.astype(BF16)
    within = jnp.einsum("hkts,hksp->hktp", weighted, x16, preferred_element_type=F32)
    last_w = jnp.exp(totals[..., None] - prefix)
    scaled = (xf * last_w[..., None]).astype(BF16)
    states = jnp.einsum("hksp,ksn->hkpn", scaled, b16, preferred_element_type=F32)

    gain = jnp.exp(totals)
    local = jnp.zeros(states.shape[:1] + states.shape[2:], F32)
    before = []
    run_log = jnp.zeros((head_count,), F32)
    for k in range(blocks):
        before.append(run_log)
        local = gain[:, k, None, None] * local + states[:, k]
        run_log = run_log + totals[:, k]
    device_total = run_log

    e_prefix = jnp.exp(prefix)
    g_scaled = gf * e_prefix[..., None]
    start_grad = jnp.einsum("hktp,ktn->hkpn", g_scaled, cf, precision=HIGHEST)
    state_grad = start_grad[:, 0]
    for k in range(1, blocks):
        state_grad = state_grad + jnp.exp(before[k])[:, None, None] * start_grad[:, k]

    incoming, adjoint = cross_device(local, state_grad, device_total, count)

    starts = [incoming]
    for k in range(blocks - 1):
        starts.append(gain[:, k, None, None] * starts[-1] + states[:, k])
    start = jnp.stack(starts, axis=1)
    carried = jnp.einsum("ktn,hkpn->hktp", cf, start, precision=HIGHEST)
    out = within + e_prefix[..., None] * carried
    outputs = out.transpose(1, 2, 0, 3).reshape(tokens, head_count * HEADDIM).astype(BF16)

    d_prefix = jnp.sum(g_scaled * carried, axis=-1)
    d_c = jnp.einsum("hktp,hkpn->ktn", g_scaled, start, precision=HIGHEST)

    lam = adjoint
    d_states = [None] * blocks
    d_totals = [None] * blocks
    for k in reversed(range(blocks)):
        d_states[k] = lam
        d_totals[k] = gain[:, k] * jnp.sum(lam * start[:, k], axis=(1, 2))
        lam = start_grad[:, k] + gain[:, k, None, None] * lam
    d_states = jnp.stack(d_states, axis=1)
    d_totals = jnp.stack(d_totals, axis=1)

    d_scaled = rounded(jnp.einsum("ksn,hkpn->hksp", bf, d_states, precision=HIGHEST))
    d_b = jnp.einsum("hksp,hkpn->ksn", scaled.astype(F32), d_states, precision=HIGHEST)
    d_x = d_scaled * last_w[..., None]
    d_last = jnp.sum(d_scaled * xf, axis=-1) * last_w
    d_prefix = d_prefix - d_last
    d_totals = d_totals + jnp.sum(d_last, axis=-1)

    d_weighted = jnp.einsum("hktp,hksp->hkts", g16, x16, preferred_element_type=F32)
    d_weighted = rounded(d_weighted)
    d_x = d_x + rounded(jnp.einsum("hkts,hktp->hksp", weighted, g16, preferred_element_type=F32))
    spread_grad = d_weighted * weighted_f
    d_prefix = d_prefix + jnp.sum(spread_grad, axis=-1) - jnp.sum(spread_grad, axis=-2)
    d_scores = jnp.sum(d_weighted * decay_mat, axis=0).astype(BF16)
    d_c = d_c + jnp.einsum("kts,ksn->ktn", d_scores, b16, preferred_element_type=F32)
    d_b = d_b + jnp.einsum("kts,ktn->ksn", d_scores, c16, preferred_element_type=F32)

    d_prefix = d_prefix.at[..., -1].add(d_totals)
    d_decay = lax.cumsum(d_prefix, axis=2, reverse=True)
    grad_decay = d_decay.transpose(1, 2, 0).reshape(tokens, head_count)
    grad_inputs = d_x.transpose(1, 2, 0, 3).reshape(tokens, head_count * HEADDIM).astype(BF16)
    grad_b, grad_c = lax.psum((d_b.reshape(tokens, STATE), d_c.reshape(tokens, STATE)), "head")
    return (outputs, grad_inputs, grad_decay, grad_b, grad_c)


def solution(mesh):
    count = mesh.shape["seq"]
    placed = (P("seq", "head"), P("seq", "head"), P("seq", None), P("seq", None), P("seq", "head"))

    def body(inputs, log_decay, b_proj, c_proj, grad_out):
        return shards(inputs, log_decay, b_proj, c_proj, grad_out, count)

    return jax.shard_map(
        body,
        mesh=mesh,
        in_specs=placed,
        out_specs=(
            P("seq", "head"),
            P("seq", "head"),
            P("seq", "head"),
            P("seq", None),
            P("seq", None),
        ),
        check_vma=False,
    )
```

```python
import jax
import jax.numpy as jnp
from jax import lax
from jax.sharding import PartitionSpec as P

HEADDIM = 64
STATE = 128
BLOCK = 256

F32 = jnp.float32
BF16 = jnp.bfloat16
HIGHEST = lax.Precision.HIGHEST


def rounded(values):
    return values.astype(BF16).astype(F32)


def cross_device(final, state_grad, total, count):
    heads, width, state = final.shape
    rows = heads * width
    if count == 1:
        zero = jnp.zeros_like(final)
        return zero, zero
    share = rows // count
    piece = share * state
    lanes = -(-heads // 128) * 128
    logs = jnp.pad(total, (0, lanes - heads))
    payload = jnp.concatenate(
        [
            final.reshape(count, piece),
            state_grad.reshape(count, piece),
            jnp.broadcast_to(logs[None], (count, lanes)),
        ],
        axis=1,
    )
    got = lax.all_to_all(payload, "seq", 0, 0, tiled=True)
    ends = got[:, :piece].reshape(count, share, state)
    grads = got[:, piece : 2 * piece].reshape(count, share, state)
    totals = got[:, 2 * piece : 2 * piece + heads]
    place = lax.axis_index("seq")
    row_heads = (place * share + jnp.arange(share)) // width
    gains = jnp.exp(jnp.take(totals, row_heads, axis=1))[:, :, None]
    zero = jnp.zeros((share, state), F32)
    ahead = [zero]
    for j in range(count - 1):
        ahead.append(gains[j] * ahead[-1] + ends[j])
    behind = [zero]
    for j in range(count - 1, 0, -1):
        behind.append(grads[j] + gains[j] * behind[-1])
    behind = behind[::-1]
    back = jnp.concatenate(
        [jnp.stack(ahead).reshape(count, piece), jnp.stack(behind).reshape(count, piece)], axis=1
    )
    back = lax.all_to_all(back, "seq", 0, 0, tiled=True)
    incoming = back[:, :piece].reshape(heads, width, state)
    adjoint = back[:, piece:].reshape(heads, width, state)
    return incoming, adjoint


def head_sum(parts, size):
    if size & (size - 1):
        return lax.psum(parts, "head")
    step = 1
    while step < size:
        pairs = [(i, i ^ step) for i in range(size)]
        parts = jax.tree.map(lambda a: a + lax.ppermute(a, "head", pairs), parts)
        step *= 2
    return parts


def shards(inputs, log_decay, b_proj, c_proj, grad_out, count, head_size):
    tokens, head_count = log_decay.shape
    blocks = tokens // BLOCK
    x16 = inputs.reshape(blocks, BLOCK, head_count, HEADDIM).transpose(2, 0, 1, 3)
    g16 = grad_out.reshape(blocks, BLOCK, head_count, HEADDIM).transpose(2, 0, 1, 3)
    xf = x16.astype(F32)
    gf = g16.astype(F32)
    decay = log_decay.reshape(blocks, BLOCK, head_count).transpose(2, 0, 1)
    b16 = b_proj.reshape(blocks, BLOCK, STATE)
    c16 = c_proj.reshape(blocks, BLOCK, STATE)
    bf = b16.astype(F32)
    cf = c16.astype(F32)

    prefix = jnp.cumsum(decay, axis=-1)
    totals = prefix[..., -1]
    causal = jnp.tril(jnp.ones((BLOCK, BLOCK), dtype=bool))
    scores = jnp.einsum("ktn,ksn->kts", c16, b16, preferred_element_type=F32)
    spread = prefix[..., :, None] - prefix[..., None, :]
    decay_mat = jnp.where(causal, jnp.exp(jnp.where(causal, spread, 0.0)), 0.0)
    weighted_f = scores[None] * decay_mat
    weighted = weighted_f.astype(BF16)
    within = jnp.einsum("hkts,hksp->hktp", weighted, x16, preferred_element_type=F32)
    last_w = jnp.exp(totals[..., None] - prefix)
    scaled = (xf * last_w[..., None]).astype(BF16)
    states = jnp.einsum("hksp,ksn->hkpn", scaled, b16, preferred_element_type=F32)

    gain = jnp.exp(totals)
    local = jnp.zeros(states.shape[:1] + states.shape[2:], F32)
    before = []
    run_log = jnp.zeros((head_count,), F32)
    for k in range(blocks):
        before.append(run_log)
        local = gain[:, k, None, None] * local + states[:, k]
        run_log = run_log + totals[:, k]
    device_total = run_log

    e_prefix = jnp.exp(prefix)
    g_scaled = gf * e_prefix[..., None]
    start_grad = jnp.einsum("hktp,ktn->hkpn", g_scaled, cf, precision=HIGHEST)
    state_grad = start_grad[:, 0]
    for k in range(1, blocks):
        state_grad = state_grad + jnp.exp(before[k])[:, None, None] * start_grad[:, k]

    incoming, adjoint = cross_device(local, state_grad, device_total, count)

    starts = [incoming]
    for k in range(blocks - 1):
        starts.append(gain[:, k, None, None] * starts[-1] + states[:, k])
    start = jnp.stack(starts, axis=1)
    carried = jnp.einsum("ktn,hkpn->hktp", cf, start, precision=HIGHEST)
    out = within + e_prefix[..., None] * carried
    outputs = out.transpose(1, 2, 0, 3).reshape(tokens, head_count * HEADDIM).astype(BF16)

    d_prefix = jnp.sum(g_scaled * carried, axis=-1)
    d_c = jnp.einsum("hktp,hkpn->ktn", g_scaled, start, precision=HIGHEST)

    lam = adjoint
    d_states = [None] * blocks
    d_totals = [None] * blocks
    for k in reversed(range(blocks)):
        d_states[k] = lam
        d_totals[k] = gain[:, k] * jnp.sum(lam * start[:, k], axis=(1, 2))
        lam = start_grad[:, k] + gain[:, k, None, None] * lam
    d_states = jnp.stack(d_states, axis=1)
    d_totals = jnp.stack(d_totals, axis=1)

    d_scaled = rounded(jnp.einsum("ksn,hkpn->hksp", bf, d_states, precision=HIGHEST))
    d_b = jnp.einsum("hksp,hkpn->ksn", scaled.astype(F32), d_states, precision=HIGHEST)
    d_x = d_scaled * last_w[..., None]
    d_last = jnp.sum(d_scaled * xf, axis=-1) * last_w
    d_prefix = d_prefix - d_last
    d_totals = d_totals + jnp.sum(d_last, axis=-1)

    d_weighted = jnp.einsum("hktp,hksp->hkts", g16, x16, preferred_element_type=F32)
    d_weighted = rounded(d_weighted)
    d_x = d_x + rounded(jnp.einsum("hkts,hktp->hksp", weighted, g16, preferred_element_type=F32))
    spread_grad = d_weighted * weighted_f
    d_prefix = d_prefix + jnp.sum(spread_grad, axis=-1) - jnp.sum(spread_grad, axis=-2)
    d_scores = jnp.sum(d_weighted * decay_mat, axis=0).astype(BF16)
    d_c = d_c + jnp.einsum("kts,ksn->ktn", d_scores, b16, preferred_element_type=F32)
    d_b = d_b + jnp.einsum("kts,ktn->ksn", d_scores, c16, preferred_element_type=F32)

    d_prefix = d_prefix.at[..., -1].add(d_totals)
    d_decay = lax.cumsum(d_prefix, axis=2, reverse=True)
    grad_decay = d_decay.transpose(1, 2, 0).reshape(tokens, head_count)
    grad_inputs = d_x.transpose(1, 2, 0, 3).reshape(tokens, head_count * HEADDIM).astype(BF16)
    grad_b, grad_c = head_sum((d_b.reshape(tokens, STATE), d_c.reshape(tokens, STATE)), head_size)
    return (outputs, grad_inputs, grad_decay, grad_b, grad_c)


def solution(mesh):
    count = mesh.shape["seq"]
    head_size = mesh.shape["head"]
    placed = (P("seq", "head"), P("seq", "head"), P("seq", None), P("seq", None), P("seq", "head"))

    def body(inputs, log_decay, b_proj, c_proj, grad_out):
        return shards(inputs, log_decay, b_proj, c_proj, grad_out, count, head_size)

    return jax.shard_map(
        body,
        mesh=mesh,
        in_specs=placed,
        out_specs=(
            P("seq", "head"),
            P("seq", "head"),
            P("seq", "head"),
            P("seq", None),
            P("seq", None),
        ),
        check_vma=False,
    )
```

```python
import jax
import jax.numpy as jnp
from jax import lax
from jax.sharding import PartitionSpec as P

HEADDIM = 64
STATE = 128
BLOCK = 256

F32 = jnp.float32
BF16 = jnp.bfloat16
HIGHEST = lax.Precision.HIGHEST


def rounded(values):
    return values.astype(BF16).astype(F32)


def gather_rows(final, state_grad, total, count):
    heads, width, state = final.shape
    piece = heads * width * state // count
    lanes = -(-heads // 128) * 128
    logs = jnp.pad(total, (0, lanes - heads))
    payload = jnp.concatenate(
        [
            final.reshape(count, piece),
            state_grad.reshape(count, piece),
            jnp.broadcast_to(logs[None], (count, lanes)),
        ],
        axis=1,
    )
    return lax.all_to_all(payload, "seq", 0, 0, tiled=True)


def scan_rows(got, heads, width, count):
    share = heads * width // count
    piece = share * STATE
    ends = got[:, :piece].reshape(count, share, STATE)
    grads = got[:, piece : 2 * piece].reshape(count, share, STATE)
    totals = got[:, 2 * piece : 2 * piece + heads]
    place = lax.axis_index("seq")
    row_heads = (place * share + jnp.arange(share)) // width
    logs = jnp.take(totals, row_heads, axis=1)
    order = jnp.arange(count)
    between = (order[None, :, None] < order[None, None, :]) & (order[None, None, :] < order[:, None, None])
    spans = jnp.einsum("jik,kr->jir", between.astype(F32), logs, precision=HIGHEST)
    coef = jnp.where((order[None, :] < order[:, None])[:, :, None], jnp.exp(spans), 0.0)
    ahead = jnp.sum(coef[:, :, :, None] * ends[None], axis=1)
    behind = jnp.sum(coef[:, :, :, None] * grads[:, None], axis=0)
    return ahead.reshape(count, piece), behind.reshape(count, piece)


def send_back(rows, heads, width):
    back = lax.all_to_all(rows, "seq", 0, 0, tiled=True)
    return back.reshape(heads, width, STATE)


def head_sum(parts, size):
    if size & (size - 1):
        return lax.psum(parts, "head")
    step = 1
    while step < size:
        pairs = [(i, i ^ step) for i in range(size)]
        parts = jax.tree.map(lambda a: a + lax.ppermute(a, "head", pairs), parts)
        step *= 2
    return parts


def shards(inputs, log_decay, b_proj, c_proj, grad_out, count, head_size):
    tokens, head_count = log_decay.shape
    blocks = tokens // BLOCK
    x16 = inputs.reshape(blocks, BLOCK, head_count, HEADDIM).transpose(2, 0, 1, 3)
    g16 = grad_out.reshape(blocks, BLOCK, head_count, HEADDIM).transpose(2, 0, 1, 3)
    xf = x16.astype(F32)
    gf = g16.astype(F32)
    decay = log_decay.reshape(blocks, BLOCK, head_count).transpose(2, 0, 1)
    b16 = b_proj.reshape(blocks, BLOCK, STATE)
    c16 = c_proj.reshape(blocks, BLOCK, STATE)
    bf = b16.astype(F32)
    cf = c16.astype(F32)

    prefix = jnp.cumsum(decay, axis=-1)
    totals = prefix[..., -1]
    causal = jnp.tril(jnp.ones((BLOCK, BLOCK), dtype=bool))
    scores = jnp.einsum("ktn,ksn->kts", c16, b16, preferred_element_type=F32)
    spread = prefix[..., :, None] - prefix[..., None, :]
    decay_mat = jnp.where(causal, jnp.exp(jnp.where(causal, spread, 0.0)), 0.0)
    last_w = jnp.exp(totals[..., None] - prefix)
    scaled = (xf * last_w[..., None]).astype(BF16)
    states = jnp.einsum("hksp,ksn->hkpn", scaled, b16, preferred_element_type=F32)

    gain = jnp.exp(totals)
    local = jnp.zeros(states.shape[:1] + states.shape[2:], F32)
    before = []
    run_log = jnp.zeros((head_count,), F32)
    for k in range(blocks):
        before.append(run_log)
        local = gain[:, k, None, None] * local + states[:, k]
        run_log = run_log + totals[:, k]
    device_total = run_log

    e_prefix = jnp.exp(prefix)
    g_scaled = gf * e_prefix[..., None]
    start_grad = jnp.einsum("hktp,ktn->hkpn", g_scaled, cf, precision=HIGHEST)
    state_grad = start_grad[:, 0]
    for k in range(1, blocks):
        state_grad = state_grad + jnp.exp(before[k])[:, None, None] * start_grad[:, k]

    if count > 1:
        got = gather_rows(local, state_grad, device_total, count)

    weighted_f = scores[None] * decay_mat
    weighted = weighted_f.astype(BF16)
    within = jnp.einsum("hkts,hksp->hktp", weighted, x16, preferred_element_type=F32)
    d_weighted = jnp.einsum("hktp,hksp->hkts", g16, x16, preferred_element_type=F32)
    d_weighted = rounded(d_weighted)
    d_x_within = rounded(jnp.einsum("hkts,hktp->hksp", weighted, g16, preferred_element_type=F32))
    spread_grad = d_weighted * weighted_f
    d_prefix_within = jnp.sum(spread_grad, axis=-1) - jnp.sum(spread_grad, axis=-2)
    d_scores = jnp.sum(d_weighted * decay_mat, axis=0).astype(BF16)
    d_c_scores = jnp.einsum("kts,ksn->ktn", d_scores, b16, preferred_element_type=F32)
    d_b_scores = jnp.einsum("kts,ktn->ksn", d_scores, c16, preferred_element_type=F32)

    if count > 1:
        got, within, d_x_within, d_prefix_within, d_c_scores, d_b_scores = lax.optimization_barrier(
            (got, within, d_x_within, d_prefix_within, d_c_scores, d_b_scores)
        )
        ahead, behind = scan_rows(got, head_count, HEADDIM, count)
        incoming = send_back(ahead, head_count, HEADDIM)
        adjoint = send_back(behind, head_count, HEADDIM)
    else:
        incoming = jnp.zeros_like(local)
        adjoint = jnp.zeros_like(local)

    starts = [incoming]
    for k in range(blocks - 1):
        starts.append(gain[:, k, None, None] * starts[-1] + states[:, k])
    start = jnp.stack(starts, axis=1)
    carried = jnp.einsum("ktn,hkpn->hktp", cf, start, precision=HIGHEST)
    out = within + e_prefix[..., None] * carried
    outputs = out.transpose(1, 2, 0, 3).reshape(tokens, head_count * HEADDIM).astype(BF16)

    d_prefix = jnp.sum(g_scaled * carried, axis=-1) + d_prefix_within
    d_c = jnp.einsum("hktp,hkpn->ktn", g_scaled, start, precision=HIGHEST) + d_c_scores

    lam = adjoint
    d_states = [None] * blocks
    d_totals = [None] * blocks
    for k in reversed(range(blocks)):
        d_states[k] = lam
        d_totals[k] = gain[:, k] * jnp.sum(lam * start[:, k], axis=(1, 2))
        lam = start_grad[:, k] + gain[:, k, None, None] * lam
    d_states = jnp.stack(d_states, axis=1)
    d_totals = jnp.stack(d_totals, axis=1)

    d_scaled = rounded(jnp.einsum("ksn,hkpn->hksp", bf, d_states, precision=HIGHEST))
    d_b = jnp.einsum("hksp,hkpn->ksn", scaled.astype(F32), d_states, precision=HIGHEST) + d_b_scores
    d_x = d_scaled * last_w[..., None] + d_x_within
    d_last = jnp.sum(d_scaled * xf, axis=-1) * last_w
    d_prefix = d_prefix - d_last
    d_totals = d_totals + jnp.sum(d_last, axis=-1)

    d_prefix = d_prefix.at[..., -1].add(d_totals)
    d_decay = lax.cumsum(d_prefix, axis=2, reverse=True)
    grad_decay = d_decay.transpose(1, 2, 0).reshape(tokens, head_count)
    grad_inputs = d_x.transpose(1, 2, 0, 3).reshape(tokens, head_count * HEADDIM).astype(BF16)
    grad_b, grad_c = head_sum((d_b.reshape(tokens, STATE), d_c.reshape(tokens, STATE)), head_size)
    return (outputs, grad_inputs, grad_decay, grad_b, grad_c)


def solution(mesh):
    count = mesh.shape["seq"]
    head_size = mesh.shape["head"]
    placed = (P("seq", "head"), P("seq", "head"), P("seq", None), P("seq", None), P("seq", "head"))

    def body(inputs, log_decay, b_proj, c_proj, grad_out):
        return shards(inputs, log_decay, b_proj, c_proj, grad_out, count, head_size)

    return jax.shard_map(
        body,
        mesh=mesh,
        in_specs=placed,
        out_specs=(
            P("seq", "head"),
            P("seq", "head"),
            P("seq", "head"),
            P("seq", None),
            P("seq", None),
        ),
        check_vma=False,
    )
```

```python
import jax
import jax.numpy as jnp
from jax import lax
from jax.sharding import PartitionSpec as P

HEADDIM = 64
STATE = 128
BLOCK = 256

F32 = jnp.float32
BF16 = jnp.bfloat16
HIGHEST = lax.Precision.HIGHEST


def rounded(values):
    return values.astype(BF16).astype(F32)


def gather_rows(final, state_grad, total, count):
    heads, width, state = final.shape
    share = heads * width // count
    spare = -(-heads // (8 * state)) * 8
    logs = jnp.pad(total, (0, spare * state - heads)).reshape(spare, state)
    payload = jnp.concatenate(
        [
            final.reshape(count, share, state),
            state_grad.reshape(count, share, state),
            jnp.broadcast_to(logs[None], (count, spare, state)),
        ],
        axis=1,
    )
    return lax.all_to_all(payload, "seq", 0, 0, tiled=True)


def scan_rows(got, heads, width, count):
    share = heads * width // count
    ends = got[:, :share]
    grads = got[:, share : 2 * share]
    totals = got[:, 2 * share :].reshape(count, -1)[:, :heads]
    place = lax.axis_index("seq")
    row_heads = (place * share + jnp.arange(share)) // width
    logs = jnp.take(totals, row_heads, axis=1)
    order = jnp.arange(count)
    between = (order[None, :, None] < order[None, None, :]) & (order[None, None, :] < order[:, None, None])
    spans = jnp.einsum("jik,kr->jir", between.astype(F32), logs, precision=HIGHEST)
    coef = jnp.where((order[None, :] < order[:, None])[:, :, None], jnp.exp(spans), 0.0)
    ahead = jnp.sum(coef[:, :, :, None] * ends[None], axis=1)
    behind = jnp.sum(coef[:, :, :, None] * grads[:, None], axis=0)
    return jnp.concatenate([ahead, behind], axis=1)


def send_back(rows, heads, width, count):
    share = heads * width // count
    back = lax.all_to_all(rows, "seq", 0, 0, tiled=True)
    incoming = back[:, :share].reshape(heads, width, STATE)
    adjoint = back[:, share:].reshape(heads, width, STATE)
    return incoming, adjoint


def head_sum(parts, size):
    if size & (size - 1):
        return lax.psum(parts, "head")
    step = 1
    while step < size:
        pairs = [(i, i ^ step) for i in range(size)]
        parts = jax.tree.map(lambda a: a + lax.ppermute(a, "head", pairs), parts)
        step *= 2
    return parts


def shards(inputs, log_decay, b_proj, c_proj, grad_out, count, head_size):
    tokens, head_count = log_decay.shape
    blocks = tokens // BLOCK
    x16 = inputs.reshape(blocks, BLOCK, head_count, HEADDIM).transpose(2, 0, 1, 3)
    g16 = grad_out.reshape(blocks, BLOCK, head_count, HEADDIM).transpose(2, 0, 1, 3)
    xf = x16.astype(F32)
    gf = g16.astype(F32)
    decay = log_decay.reshape(blocks, BLOCK, head_count).transpose(2, 0, 1)
    b16 = b_proj.reshape(blocks, BLOCK, STATE)
    c16 = c_proj.reshape(blocks, BLOCK, STATE)
    bf = b16.astype(F32)
    cf = c16.astype(F32)

    prefix = jnp.cumsum(decay, axis=-1)
    totals = prefix[..., -1]
    causal = jnp.tril(jnp.ones((BLOCK, BLOCK), dtype=bool))
    scores = jnp.einsum("ktn,ksn->kts", c16, b16, preferred_element_type=F32)
    spread = prefix[..., :, None] - prefix[..., None, :]
    decay_mat = jnp.where(causal, jnp.exp(jnp.where(causal, spread, 0.0)), 0.0)
    last_w = jnp.exp(totals[..., None] - prefix)
    scaled = (xf * last_w[..., None]).astype(BF16)
    states = jnp.einsum("hksp,ksn->hkpn", scaled, b16, preferred_element_type=F32)

    gain = jnp.exp(totals)
    local = jnp.zeros(states.shape[:1] + states.shape[2:], F32)
    before = []
    run_log = jnp.zeros((head_count,), F32)
    for k in range(blocks):
        before.append(run_log)
        local = gain[:, k, None, None] * local + states[:, k]
        run_log = run_log + totals[:, k]
    device_total = run_log

    e_prefix = jnp.exp(prefix)
    g_scaled = gf * e_prefix[..., None]
    start_grad = jnp.einsum("hktp,ktn->hkpn", g_scaled, cf, precision=HIGHEST)
    state_grad = start_grad[:, 0]
    for k in range(1, blocks):
        state_grad = state_grad + jnp.exp(before[k])[:, None, None] * start_grad[:, k]

    if count > 1:
        got = gather_rows(local, state_grad, device_total, count)

    weighted_f = scores[None] * decay_mat
    weighted = weighted_f.astype(BF16)
    within = jnp.einsum("hkts,hksp->hktp", weighted, x16, preferred_element_type=F32)
    d_weighted = jnp.einsum("hktp,hksp->hkts", g16, x16, preferred_element_type=F32)
    d_weighted = rounded(d_weighted)
    d_x_within = rounded(jnp.einsum("hkts,hktp->hksp", weighted, g16, preferred_element_type=F32))
    spread_grad = d_weighted * weighted_f
    d_prefix_within = jnp.sum(spread_grad, axis=-1) - jnp.sum(spread_grad, axis=-2)
    d_scores = jnp.sum(d_weighted * decay_mat, axis=0).astype(BF16)
    d_c_scores = jnp.einsum("kts,ksn->ktn", d_scores, b16, preferred_element_type=F32)
    d_b_scores = jnp.einsum("kts,ktn->ksn", d_scores, c16, preferred_element_type=F32)

    if count > 1:
        got, within, d_x_within, d_prefix_within, d_c_scores, d_b_scores = lax.optimization_barrier(
            (got, within, d_x_within, d_prefix_within, d_c_scores, d_b_scores)
        )
        rows = scan_rows(got, head_count, HEADDIM, count)
        incoming, adjoint = send_back(rows, head_count, HEADDIM, count)
    else:
        incoming = jnp.zeros_like(local)
        adjoint = jnp.zeros_like(local)

    starts = [incoming]
    for k in range(blocks - 1):
        starts.append(gain[:, k, None, None] * starts[-1] + states[:, k])
    start = jnp.stack(starts, axis=1)
    carried = jnp.einsum("ktn,hkpn->hktp", cf, start, precision=HIGHEST)
    out = within + e_prefix[..., None] * carried
    outputs = out.transpose(1, 2, 0, 3).reshape(tokens, head_count * HEADDIM).astype(BF16)

    d_prefix = jnp.sum(g_scaled * carried, axis=-1) + d_prefix_within
    d_c = jnp.einsum("hktp,hkpn->ktn", g_scaled, start, precision=HIGHEST) + d_c_scores

    lam = adjoint
    d_states = [None] * blocks
    d_totals = [None] * blocks
    for k in reversed(range(blocks)):
        d_states[k] = lam
        d_totals[k] = gain[:, k] * jnp.sum(lam * start[:, k], axis=(1, 2))
        lam = start_grad[:, k] + gain[:, k, None, None] * lam
    d_states = jnp.stack(d_states, axis=1)
    d_totals = jnp.stack(d_totals, axis=1)

    d_scaled = rounded(jnp.einsum("ksn,hkpn->hksp", bf, d_states, precision=HIGHEST))
    d_b = jnp.einsum("hksp,hkpn->ksn", scaled.astype(F32), d_states, precision=HIGHEST) + d_b_scores
    d_x = d_scaled * last_w[..., None] + d_x_within
    d_last = jnp.sum(d_scaled * xf, axis=-1) * last_w
    d_prefix = d_prefix - d_last
    d_totals = d_totals + jnp.sum(d_last, axis=-1)

    d_prefix = d_prefix.at[..., -1].add(d_totals)
    d_decay = lax.cumsum(d_prefix, axis=2, reverse=True)
    grad_decay = d_decay.transpose(1, 2, 0).reshape(tokens, head_count)
    grad_inputs = d_x.transpose(1, 2, 0, 3).reshape(tokens, head_count * HEADDIM).astype(BF16)
    grad_b, grad_c = head_sum((d_b.reshape(tokens, STATE), d_c.reshape(tokens, STATE)), head_size)
    return (outputs, grad_inputs, grad_decay, grad_b, grad_c)


def solution(mesh):
    count = mesh.shape["seq"]
    head_size = mesh.shape["head"]
    placed = (P("seq", "head"), P("seq", "head"), P("seq", None), P("seq", None), P("seq", "head"))

    def body(inputs, log_decay, b_proj, c_proj, grad_out):
        return shards(inputs, log_decay, b_proj, c_proj, grad_out, count, head_size)

    return jax.shard_map(
        body,
        mesh=mesh,
        in_specs=placed,
        out_specs=(
            P("seq", "head"),
            P("seq", "head"),
            P("seq", "head"),
            P("seq", None),
            P("seq", None),
        ),
        check_vma=False,
    )
```

```python
import jax
import jax.numpy as jnp
from jax import lax
from jax.sharding import Mesh, PartitionSpec as P

HEADDIM = 64
STATE = 128
BLOCK = 256

F32 = jnp.float32
BF16 = jnp.bfloat16
HIGHEST = lax.Precision.HIGHEST


def rounded(values):
    return values.astype(BF16).astype(F32)


def gather_rows(final, state_grad, total, count):
    heads, width, state = final.shape
    share = heads * width // count
    spare = -(-heads // (8 * state)) * 8
    logs = jnp.pad(total, (0, spare * state - heads)).reshape(spare, state)
    payload = jnp.concatenate(
        [
            final.reshape(count, share, state),
            state_grad.reshape(count, share, state),
            jnp.broadcast_to(logs[None], (count, spare, state)),
        ],
        axis=1,
    )
    return lax.all_to_all(payload, "lo", 0, 0, tiled=True)


def spans_of(mask, logs):
    return jnp.exp(jnp.einsum("...k,kr->...r", mask.astype(F32), logs, precision=HIGHEST))


def scan_rows(got, heads, width, count, split):
    share = heads * width // count
    ends = got[:, :share]
    grads = got[:, share : 2 * share]
    totals = got[:, 2 * share :].reshape(count, -1)[:, :heads]
    place = lax.axis_index("lo")
    row_heads = (place * share + jnp.arange(share)) // width
    logs = jnp.take(totals, row_heads, axis=1)
    order = jnp.arange(count)
    lower = order[None, :] < order[:, None]
    between = lower.T[None, :, :] & lower[:, None, :]
    coef = jnp.where(lower[:, :, None], spans_of(between, logs), 0.0)
    ahead = jnp.sum(coef[:, :, :, None] * ends[None], axis=1)
    behind = jnp.sum(coef[:, :, :, None] * grads[:, None], axis=0)
    if split > 1:
        from_start = spans_of(lower, logs)[:, :, None]
        to_end = spans_of(lower.T, logs)[:, :, None]
        end_state = jnp.exp(logs[-1])[:, None] * ahead[-1] + ends[-1]
        start_grad = jnp.exp(logs[0])[:, None] * behind[0] + grads[0]
        side = lax.axis_index("hi")
        sent = jnp.concatenate([end_state, start_grad], axis=0)
        got_side = lax.ppermute(sent, "hi", [(0, 1), (1, 0)])
        ahead = ahead + jnp.where(side == 1, from_start * got_side[None, :share], 0.0)
        behind = behind + jnp.where(side == 0, to_end * got_side[None, share:], 0.0)
    return jnp.concatenate([ahead, behind], axis=1)


def send_back(rows, heads, width, count):
    share = heads * width // count
    back = lax.all_to_all(rows, "lo", 0, 0, tiled=True)
    incoming = back[:, :share].reshape(heads, width, STATE)
    adjoint = back[:, share:].reshape(heads, width, STATE)
    return incoming, adjoint


def head_sum(parts, size):
    if size & (size - 1):
        return lax.psum(parts, "head")
    step = 1
    while step < size:
        pairs = [(i, i ^ step) for i in range(size)]
        parts = jax.tree.map(lambda a: a + lax.ppermute(a, "head", pairs), parts)
        step *= 2
    return parts


def shards(inputs, log_decay, b_proj, c_proj, grad_out, count, head_size, split):
    tokens, head_count = log_decay.shape
    blocks = tokens // BLOCK
    x16 = inputs.reshape(blocks, BLOCK, head_count, HEADDIM).transpose(2, 0, 1, 3)
    g16 = grad_out.reshape(blocks, BLOCK, head_count, HEADDIM).transpose(2, 0, 1, 3)
    xf = x16.astype(F32)
    gf = g16.astype(F32)
    decay = log_decay.reshape(blocks, BLOCK, head_count).transpose(2, 0, 1)
    b16 = b_proj.reshape(blocks, BLOCK, STATE)
    c16 = c_proj.reshape(blocks, BLOCK, STATE)
    bf = b16.astype(F32)
    cf = c16.astype(F32)

    prefix = jnp.cumsum(decay, axis=-1)
    totals = prefix[..., -1]
    causal = jnp.tril(jnp.ones((BLOCK, BLOCK), dtype=bool))
    scores = jnp.einsum("ktn,ksn->kts", c16, b16, preferred_element_type=F32)
    spread = prefix[..., :, None] - prefix[..., None, :]
    decay_mat = jnp.where(causal, jnp.exp(jnp.where(causal, spread, 0.0)), 0.0)
    last_w = jnp.exp(totals[..., None] - prefix)
    scaled = (xf * last_w[..., None]).astype(BF16)
    states = jnp.einsum("hksp,ksn->hkpn", scaled, b16, preferred_element_type=F32)

    gain = jnp.exp(totals)
    local = jnp.zeros(states.shape[:1] + states.shape[2:], F32)
    before = []
    run_log = jnp.zeros((head_count,), F32)
    for k in range(blocks):
        before.append(run_log)
        local = gain[:, k, None, None] * local + states[:, k]
        run_log = run_log + totals[:, k]
    device_total = run_log

    e_prefix = jnp.exp(prefix)
    g_scaled = gf * e_prefix[..., None]
    start_grad = jnp.einsum("hktp,ktn->hkpn", g_scaled, cf, precision=HIGHEST)
    state_grad = start_grad[:, 0]
    for k in range(1, blocks):
        state_grad = state_grad + jnp.exp(before[k])[:, None, None] * start_grad[:, k]

    if count > 1:
        got = gather_rows(local, state_grad, device_total, count)

    weighted_f = scores[None] * decay_mat
    weighted = weighted_f.astype(BF16)
    within = jnp.einsum("hkts,hksp->hktp", weighted, x16, preferred_element_type=F32)
    d_weighted = jnp.einsum("hktp,hksp->hkts", g16, x16, preferred_element_type=F32)
    d_weighted = rounded(d_weighted)
    d_x_within = rounded(jnp.einsum("hkts,hktp->hksp", weighted, g16, preferred_element_type=F32))
    spread_grad = d_weighted * weighted_f
    d_prefix_within = jnp.sum(spread_grad, axis=-1) - jnp.sum(spread_grad, axis=-2)
    d_scores = jnp.sum(d_weighted * decay_mat, axis=0).astype(BF16)
    d_c_scores = jnp.einsum("kts,ksn->ktn", d_scores, b16, preferred_element_type=F32)
    d_b_scores = jnp.einsum("kts,ktn->ksn", d_scores, c16, preferred_element_type=F32)

    if count > 1:
        got, within, d_x_within, d_prefix_within, d_c_scores, d_b_scores = lax.optimization_barrier(
            (got, within, d_x_within, d_prefix_within, d_c_scores, d_b_scores)
        )
        rows = scan_rows(got, head_count, HEADDIM, count, split)
        incoming, adjoint = send_back(rows, head_count, HEADDIM, count)
    else:
        incoming = jnp.zeros_like(local)
        adjoint = jnp.zeros_like(local)

    starts = [incoming]
    for k in range(blocks - 1):
        starts.append(gain[:, k, None, None] * starts[-1] + states[:, k])
    start = jnp.stack(starts, axis=1)
    carried = jnp.einsum("ktn,hkpn->hktp", cf, start, precision=HIGHEST)
    out = within + e_prefix[..., None] * carried
    outputs = out.transpose(1, 2, 0, 3).reshape(tokens, head_count * HEADDIM).astype(BF16)

    d_prefix = jnp.sum(g_scaled * carried, axis=-1) + d_prefix_within
    d_c = jnp.einsum("hktp,hkpn->ktn", g_scaled, start, precision=HIGHEST) + d_c_scores

    lam = adjoint
    d_states = [None] * blocks
    d_totals = [None] * blocks
    for k in reversed(range(blocks)):
        d_states[k] = lam
        d_totals[k] = gain[:, k] * jnp.sum(lam * start[:, k], axis=(1, 2))
        lam = start_grad[:, k] + gain[:, k, None, None] * lam
    d_states = jnp.stack(d_states, axis=1)
    d_totals = jnp.stack(d_totals, axis=1)

    d_scaled = rounded(jnp.einsum("ksn,hkpn->hksp", bf, d_states, precision=HIGHEST))
    d_b = jnp.einsum("hksp,hkpn->ksn", scaled.astype(F32), d_states, precision=HIGHEST) + d_b_scores
    d_x = d_scaled * last_w[..., None] + d_x_within
    d_last = jnp.sum(d_scaled * xf, axis=-1) * last_w
    d_prefix = d_prefix - d_last
    d_totals = d_totals + jnp.sum(d_last, axis=-1)

    d_prefix = d_prefix.at[..., -1].add(d_totals)
    d_decay = lax.cumsum(d_prefix, axis=2, reverse=True)
    grad_decay = d_decay.transpose(1, 2, 0).reshape(tokens, head_count)
    grad_inputs = d_x.transpose(1, 2, 0, 3).reshape(tokens, head_count * HEADDIM).astype(BF16)
    grad_b, grad_c = head_sum((d_b.reshape(tokens, STATE), d_c.reshape(tokens, STATE)), head_size)
    return (outputs, grad_inputs, grad_decay, grad_b, grad_c)


def solution(mesh):
    seq_size = mesh.shape["seq"]
    head_size = mesh.shape["head"]
    split = 2 if seq_size % 4 == 0 else 1
    count = seq_size // split
    grid = Mesh(mesh.devices.reshape(split, count, head_size), ("hi", "lo", "head"))
    seq = ("hi", "lo")
    placed = (P(seq, "head"), P(seq, "head"), P(seq, None), P(seq, None), P(seq, "head"))

    def body(inputs, log_decay, b_proj, c_proj, grad_out):
        return shards(inputs, log_decay, b_proj, c_proj, grad_out, count, head_size, split)

    return jax.shard_map(
        body,
        mesh=grid,
        in_specs=placed,
        out_specs=(P(seq, "head"), P(seq, "head"), P(seq, "head"), P(seq, None), P(seq, None)),
        check_vma=False,
    )
```

```python
import jax
import jax.numpy as jnp
from jax import lax
from jax.sharding import Mesh, PartitionSpec as P

HEADDIM = 64
STATE = 128
BLOCK = 256

F32 = jnp.float32
BF16 = jnp.bfloat16
HIGHEST = lax.Precision.HIGHEST


def rounded(values):
    return values.astype(BF16).astype(F32)


def gather_rows(final, state_grad, total, count):
    heads, width, state = final.shape
    share = heads * width // count
    spare = -(-heads // (8 * state)) * 8
    logs = jnp.pad(total, (0, spare * state - heads)).reshape(spare, state)
    payload = jnp.concatenate(
        [
            final.reshape(count, share, state),
            state_grad.reshape(count, share, state),
            jnp.broadcast_to(logs[None], (count, spare, state)),
        ],
        axis=1,
    )
    return lax.all_to_all(payload, "lo", 0, 0, tiled=True)


def spans_of(mask, logs):
    return jnp.exp(jnp.einsum("...k,kr->...r", mask.astype(F32), logs, precision=HIGHEST))


def scan_rows(got, heads, width, count, split):
    share = heads * width // count
    ends = got[:, :share]
    grads = got[:, share : 2 * share]
    totals = got[:, 2 * share :].reshape(count, -1)[:, :heads]
    place = lax.axis_index("lo")
    row_heads = (place * share + jnp.arange(share)) // width
    logs = jnp.take(totals, row_heads, axis=1)
    order = jnp.arange(count)
    lower = order[None, :] < order[:, None]
    between = lower.T[None, :, :] & lower[:, None, :]
    coef = jnp.where(lower[:, :, None], spans_of(between, logs), 0.0)
    ahead = jnp.sum(coef[:, :, :, None] * ends[None], axis=1)
    behind = jnp.sum(coef[:, :, :, None] * grads[:, None], axis=0)
    if split > 1:
        from_start = spans_of(lower, logs)[:, :, None]
        to_end = spans_of(lower.T, logs)[:, :, None]
        end_state = jnp.sum(to_end * ends, axis=0)
        start_grad = jnp.sum(from_start * grads, axis=0)
        side = lax.axis_index("hi")
        sent = jnp.concatenate([end_state, start_grad], axis=0)
        got_side = lax.ppermute(sent, "hi", [(0, 1), (1, 0)])
        ahead = ahead + jnp.where(side == 1, from_start * got_side[None, :share], 0.0)
        behind = behind + jnp.where(side == 0, to_end * got_side[None, share:], 0.0)
    return jnp.concatenate([ahead, behind], axis=1)


def send_back(rows, heads, width, count):
    share = heads * width // count
    back = lax.all_to_all(rows, "lo", 0, 0, tiled=True)
    incoming = back[:, :share].reshape(heads, width, STATE)
    adjoint = back[:, share:].reshape(heads, width, STATE)
    return incoming, adjoint


def head_sum(parts, size):
    if size & (size - 1):
        return lax.psum(parts, "head")
    step = 1
    while step < size:
        pairs = [(i, i ^ step) for i in range(size)]
        parts = jax.tree.map(lambda a: a + lax.ppermute(a, "head", pairs), parts)
        step *= 2
    return parts


def shards(inputs, log_decay, b_proj, c_proj, grad_out, count, head_size, split):
    tokens, head_count = log_decay.shape
    blocks = tokens // BLOCK
    x16 = inputs.reshape(blocks, BLOCK, head_count, HEADDIM).transpose(2, 0, 1, 3)
    g16 = grad_out.reshape(blocks, BLOCK, head_count, HEADDIM).transpose(2, 0, 1, 3)
    xf = x16.astype(F32)
    gf = g16.astype(F32)
    decay = log_decay.reshape(blocks, BLOCK, head_count).transpose(2, 0, 1)
    b16 = b_proj.reshape(blocks, BLOCK, STATE)
    c16 = c_proj.reshape(blocks, BLOCK, STATE)
    bf = b16.astype(F32)
    cf = c16.astype(F32)

    prefix = jnp.cumsum(decay, axis=-1)
    totals = prefix[..., -1]
    causal = jnp.tril(jnp.ones((BLOCK, BLOCK), dtype=bool))
    scores = jnp.einsum("ktn,ksn->kts", c16, b16, preferred_element_type=F32)
    spread = prefix[..., :, None] - prefix[..., None, :]
    decay_mat = jnp.where(causal, jnp.exp(jnp.where(causal, spread, 0.0)), 0.0)
    last_w = jnp.exp(totals[..., None] - prefix)
    scaled = (xf * last_w[..., None]).astype(BF16)
    states = jnp.einsum("hksp,ksn->hkpn", scaled, b16, preferred_element_type=F32)

    gain = jnp.exp(totals)
    local = jnp.zeros(states.shape[:1] + states.shape[2:], F32)
    before = []
    run_log = jnp.zeros((head_count,), F32)
    for k in range(blocks):
        before.append(run_log)
        local = gain[:, k, None, None] * local + states[:, k]
        run_log = run_log + totals[:, k]
    device_total = run_log

    e_prefix = jnp.exp(prefix)
    g_scaled = gf * e_prefix[..., None]
    start_grad = jnp.einsum("hktp,ktn->hkpn", g_scaled, cf, precision=HIGHEST)
    state_grad = start_grad[:, 0]
    for k in range(1, blocks):
        state_grad = state_grad + jnp.exp(before[k])[:, None, None] * start_grad[:, k]

    parts = 2 if head_count % 2 == 0 and (head_count // 2 * HEADDIM) % count == 0 else 1
    width = head_count // parts
    pieces = [slice(i * width, (i + 1) * width) for i in range(parts)]
    if count > 1:
        got = [gather_rows(local[h], state_grad[h], device_total[h], count) for h in pieces]

    weighted_f = scores[None] * decay_mat
    weighted = weighted_f.astype(BF16)
    within = jnp.einsum("hkts,hksp->hktp", weighted, x16, preferred_element_type=F32)
    d_weighted = jnp.einsum("hktp,hksp->hkts", g16, x16, preferred_element_type=F32)
    d_weighted = rounded(d_weighted)
    d_x_within = rounded(jnp.einsum("hkts,hktp->hksp", weighted, g16, preferred_element_type=F32))
    spread_grad = d_weighted * weighted_f
    d_prefix_within = jnp.sum(spread_grad, axis=-1) - jnp.sum(spread_grad, axis=-2)
    d_scores = jnp.sum(d_weighted * decay_mat, axis=0).astype(BF16)
    d_c_scores = jnp.einsum("kts,ksn->ktn", d_scores, b16, preferred_element_type=F32)
    d_b_scores = jnp.einsum("kts,ktn->ksn", d_scores, c16, preferred_element_type=F32)

    if count > 1:
        got, within, d_x_within, d_prefix_within, d_c_scores, d_b_scores = lax.optimization_barrier(
            (got, within, d_x_within, d_prefix_within, d_c_scores, d_b_scores)
        )

    def tail(h, incoming, adjoint):
        starts = [incoming]
        for k in range(blocks - 1):
            starts.append(gain[h, k, None, None] * starts[-1] + states[h, k])
        start = jnp.stack(starts, axis=1)
        carried = jnp.einsum("ktn,hkpn->hktp", cf, start, precision=HIGHEST)
        out = within[h] + e_prefix[h][..., None] * carried
        d_prefix = jnp.sum(g_scaled[h] * carried, axis=-1) + d_prefix_within[h]
        d_c = jnp.einsum("hktp,hkpn->ktn", g_scaled[h], start, precision=HIGHEST)
        lam = adjoint
        d_states = [None] * blocks
        d_totals = [None] * blocks
        for k in reversed(range(blocks)):
            d_states[k] = lam
            d_totals[k] = gain[h, k] * jnp.sum(lam * start[:, k], axis=(1, 2))
            lam = start_grad[h, k] + gain[h, k, None, None] * lam
        d_states = jnp.stack(d_states, axis=1)
        d_totals = jnp.stack(d_totals, axis=1)
        d_scaled = rounded(jnp.einsum("ksn,hkpn->hksp", bf, d_states, precision=HIGHEST))
        d_b = jnp.einsum("hksp,hkpn->ksn", scaled[h].astype(F32), d_states, precision=HIGHEST)
        d_x = d_scaled * last_w[h][..., None] + d_x_within[h]
        d_last = jnp.sum(d_scaled * xf[h], axis=-1) * last_w[h]
        d_prefix = d_prefix - d_last
        d_totals = d_totals + jnp.sum(d_last, axis=-1)
        d_prefix = d_prefix.at[..., -1].add(d_totals)
        return out, d_x, d_prefix, d_b, d_c

    results = []
    for i, h in enumerate(pieces):
        if count > 1:
            rows = scan_rows(got[i], width, HEADDIM, count, split)
            incoming, adjoint = send_back(rows, width, HEADDIM, count)
        else:
            incoming = jnp.zeros_like(local[h])
            adjoint = jnp.zeros_like(local[h])
        results.append(tail(h, incoming, adjoint))
    out = jnp.concatenate([r[0] for r in results], axis=0)
    d_x = jnp.concatenate([r[1] for r in results], axis=0)
    d_prefix = jnp.concatenate([r[2] for r in results], axis=0)
    d_b = sum(r[3] for r in results) + d_b_scores
    d_c = sum(r[4] for r in results) + d_c_scores

    outputs = out.transpose(1, 2, 0, 3).reshape(tokens, head_count * HEADDIM).astype(BF16)
    d_decay = lax.cumsum(d_prefix, axis=2, reverse=True)
    grad_decay = d_decay.transpose(1, 2, 0).reshape(tokens, head_count)
    grad_inputs = d_x.transpose(1, 2, 0, 3).reshape(tokens, head_count * HEADDIM).astype(BF16)
    grad_b, grad_c = head_sum((d_b.reshape(tokens, STATE), d_c.reshape(tokens, STATE)), head_size)
    return (outputs, grad_inputs, grad_decay, grad_b, grad_c)


def solution(mesh):
    seq_size = mesh.shape["seq"]
    head_size = mesh.shape["head"]
    split = 2 if seq_size % 4 == 0 else 1
    count = seq_size // split
    grid = Mesh(mesh.devices.reshape(split, count, head_size), ("hi", "lo", "head"))
    seq = ("hi", "lo")
    placed = (P(seq, "head"), P(seq, "head"), P(seq, None), P(seq, None), P(seq, "head"))

    def body(inputs, log_decay, b_proj, c_proj, grad_out):
        return shards(inputs, log_decay, b_proj, c_proj, grad_out, count, head_size, split)

    return jax.shard_map(
        body,
        mesh=grid,
        in_specs=placed,
        out_specs=(P(seq, "head"), P(seq, "head"), P(seq, "head"), P(seq, None), P(seq, None)),
        check_vma=False,
    )
```

```python
import jax
import jax.numpy as jnp
from jax import lax
from jax.sharding import Mesh, PartitionSpec as P

HEADDIM = 64
STATE = 128
BLOCK = 256

F32 = jnp.float32
BF16 = jnp.bfloat16
HIGHEST = lax.Precision.HIGHEST


def rounded(values):
    return values.astype(BF16).astype(F32)


def split_dot(spec, exact, wide, swap=False):
    high = wide.astype(BF16)
    low = (wide - high.astype(F32)).astype(BF16)
    exact = exact.astype(BF16)
    if swap:
        return jnp.einsum(spec, high, exact, preferred_element_type=F32) + jnp.einsum(
            spec, low, exact, preferred_element_type=F32
        )
    return jnp.einsum(spec, exact, high, preferred_element_type=F32) + jnp.einsum(
        spec, exact, low, preferred_element_type=F32
    )


def gather_rows(final, state_grad, total, count):
    heads, width, state = final.shape
    share = heads * width // count
    spare = -(-heads // (8 * state)) * 8
    logs = jnp.pad(total, (0, spare * state - heads)).reshape(spare, state)
    payload = jnp.concatenate(
        [
            final.reshape(count, share, state),
            state_grad.reshape(count, share, state),
            jnp.broadcast_to(logs[None], (count, spare, state)),
        ],
        axis=1,
    )
    return lax.all_to_all(payload, "lo", 0, 0, tiled=True)


def spans_of(mask, logs):
    return jnp.exp(jnp.einsum("...k,kr->...r", mask.astype(F32), logs, precision=HIGHEST))


def scan_rows(got, heads, width, count, split):
    share = heads * width // count
    ends = got[:, :share]
    grads = got[:, share : 2 * share]
    totals = got[:, 2 * share :].reshape(count, -1)[:, :heads]
    place = lax.axis_index("lo")
    row_heads = (place * share + jnp.arange(share)) // width
    logs = jnp.take(totals, row_heads, axis=1)
    order = jnp.arange(count)
    lower = order[None, :] < order[:, None]
    between = lower.T[None, :, :] & lower[:, None, :]
    coef = jnp.where(lower[:, :, None], spans_of(between, logs), 0.0)
    ahead = jnp.sum(coef[:, :, :, None] * ends[None], axis=1)
    behind = jnp.sum(coef[:, :, :, None] * grads[:, None], axis=0)
    if split > 1:
        from_start = spans_of(lower, logs)[:, :, None]
        to_end = spans_of(lower.T, logs)[:, :, None]
        end_state = jnp.sum(to_end * ends, axis=0)
        start_grad = jnp.sum(from_start * grads, axis=0)
        side = lax.axis_index("hi")
        sent = jnp.concatenate([end_state, start_grad], axis=0)
        got_side = lax.ppermute(sent, "hi", [(0, 1), (1, 0)])
        ahead = ahead + jnp.where(side == 1, from_start * got_side[None, :share], 0.0)
        behind = behind + jnp.where(side == 0, to_end * got_side[None, share:], 0.0)
    return jnp.concatenate([ahead, behind], axis=1)


def send_back(rows, heads, width, count):
    share = heads * width // count
    back = lax.all_to_all(rows, "lo", 0, 0, tiled=True)
    incoming = back[:, :share].reshape(heads, width, STATE)
    adjoint = back[:, share:].reshape(heads, width, STATE)
    return incoming, adjoint


def head_sum(parts, size):
    if size & (size - 1):
        return lax.psum(parts, "head")
    step = 1
    while step < size:
        pairs = [(i, i ^ step) for i in range(size)]
        parts = jax.tree.map(lambda a: a + lax.ppermute(a, "head", pairs), parts)
        step *= 2
    return parts


def shards(inputs, log_decay, b_proj, c_proj, grad_out, count, head_size, split):
    tokens, head_count = log_decay.shape
    blocks = tokens // BLOCK
    x16 = inputs.reshape(blocks, BLOCK, head_count, HEADDIM).transpose(2, 0, 1, 3)
    g16 = grad_out.reshape(blocks, BLOCK, head_count, HEADDIM).transpose(2, 0, 1, 3)
    xf = x16.astype(F32)
    gf = g16.astype(F32)
    decay = log_decay.reshape(blocks, BLOCK, head_count).transpose(2, 0, 1)
    b16 = b_proj.reshape(blocks, BLOCK, STATE)
    c16 = c_proj.reshape(blocks, BLOCK, STATE)
    bf = b16.astype(F32)
    cf = c16.astype(F32)

    prefix = jnp.cumsum(decay, axis=-1)
    totals = prefix[..., -1]
    causal = jnp.tril(jnp.ones((BLOCK, BLOCK), dtype=bool))
    scores = jnp.einsum("ktn,ksn->kts", c16, b16, preferred_element_type=F32)
    spread = prefix[..., :, None] - prefix[..., None, :]
    decay_mat = jnp.where(causal, jnp.exp(jnp.where(causal, spread, 0.0)), 0.0)
    last_w = jnp.exp(totals[..., None] - prefix)
    scaled = (xf * last_w[..., None]).astype(BF16)
    states = jnp.einsum("hksp,ksn->hkpn", scaled, b16, preferred_element_type=F32)

    gain = jnp.exp(totals)
    local = jnp.zeros(states.shape[:1] + states.shape[2:], F32)
    before = []
    run_log = jnp.zeros((head_count,), F32)
    for k in range(blocks):
        before.append(run_log)
        local = gain[:, k, None, None] * local + states[:, k]
        run_log = run_log + totals[:, k]
    device_total = run_log

    e_prefix = jnp.exp(prefix)
    g_scaled = gf * e_prefix[..., None]
    start_grad = split_dot("hktp,ktn->hkpn", c16, g_scaled, swap=True)
    state_grad = start_grad[:, 0]
    for k in range(1, blocks):
        state_grad = state_grad + jnp.exp(before[k])[:, None, None] * start_grad[:, k]

    if count > 1:
        got = gather_rows(local, state_grad, device_total, count)

    weighted_f = scores[None] * decay_mat
    weighted = weighted_f.astype(BF16)
    within = jnp.einsum("hkts,hksp->hktp", weighted, x16, preferred_element_type=F32)
    d_weighted = jnp.einsum("hktp,hksp->hkts", g16, x16, preferred_element_type=F32)
    d_weighted = rounded(d_weighted)
    d_x_within = rounded(jnp.einsum("hkts,hktp->hksp", weighted, g16, preferred_element_type=F32))
    spread_grad = d_weighted * weighted_f
    d_prefix_within = jnp.sum(spread_grad, axis=-1) - jnp.sum(spread_grad, axis=-2)
    d_scores = jnp.sum(d_weighted * decay_mat, axis=0).astype(BF16)
    d_c_scores = jnp.einsum("kts,ksn->ktn", d_scores, b16, preferred_element_type=F32)
    d_b_scores = jnp.einsum("kts,ktn->ksn", d_scores, c16, preferred_element_type=F32)

    if count > 1:
        got, within, d_x_within, d_prefix_within, d_c_scores, d_b_scores = lax.optimization_barrier(
            (got, within, d_x_within, d_prefix_within, d_c_scores, d_b_scores)
        )
        rows = scan_rows(got, head_count, HEADDIM, count, split)
        incoming, adjoint = send_back(rows, head_count, HEADDIM, count)
    else:
        incoming = jnp.zeros_like(local)
        adjoint = jnp.zeros_like(local)

    starts = [incoming]
    for k in range(blocks - 1):
        starts.append(gain[:, k, None, None] * starts[-1] + states[:, k])
    start = jnp.stack(starts, axis=1)
    carried = split_dot("ktn,hkpn->hktp", c16, start)
    out = within + e_prefix[..., None] * carried
    outputs = out.transpose(1, 2, 0, 3).reshape(tokens, head_count * HEADDIM).astype(BF16)

    d_prefix = jnp.sum(g_scaled * carried, axis=-1) + d_prefix_within
    d_c = jnp.einsum("hktp,hkpn->ktn", g_scaled, start, precision=lax.Precision.HIGH) + d_c_scores

    lam = adjoint
    d_states = [None] * blocks
    d_totals = [None] * blocks
    for k in reversed(range(blocks)):
        d_states[k] = lam
        d_totals[k] = gain[:, k] * jnp.sum(lam * start[:, k], axis=(1, 2))
        lam = start_grad[:, k] + gain[:, k, None, None] * lam
    d_states = jnp.stack(d_states, axis=1)
    d_totals = jnp.stack(d_totals, axis=1)

    d_scaled = rounded(split_dot("ksn,hkpn->hksp", b16, d_states))
    d_b = split_dot("hksp,hkpn->ksn", scaled, d_states) + d_b_scores
    d_x = d_scaled * last_w[..., None] + d_x_within
    d_last = jnp.sum(d_scaled * xf, axis=-1) * last_w
    d_prefix = d_prefix - d_last
    d_totals = d_totals + jnp.sum(d_last, axis=-1)

    d_prefix = d_prefix.at[..., -1].add(d_totals)
    d_decay = lax.cumsum(d_prefix, axis=2, reverse=True)
    grad_decay = d_decay.transpose(1, 2, 0).reshape(tokens, head_count)
    grad_inputs = d_x.transpose(1, 2, 0, 3).reshape(tokens, head_count * HEADDIM).astype(BF16)
    grad_b, grad_c = head_sum((d_b.reshape(tokens, STATE), d_c.reshape(tokens, STATE)), head_size)
    return (outputs, grad_inputs, grad_decay, grad_b, grad_c)


def solution(mesh):
    seq_size = mesh.shape["seq"]
    head_size = mesh.shape["head"]
    split = 2 if seq_size % 4 == 0 else 1
    count = seq_size // split
    grid = Mesh(mesh.devices.reshape(split, count, head_size), ("hi", "lo", "head"))
    seq = ("hi", "lo")
    placed = (P(seq, "head"), P(seq, "head"), P(seq, None), P(seq, None), P(seq, "head"))

    def body(inputs, log_decay, b_proj, c_proj, grad_out):
        return shards(inputs, log_decay, b_proj, c_proj, grad_out, count, head_size, split)

    return jax.shard_map(
        body,
        mesh=grid,
        in_specs=placed,
        out_specs=(P(seq, "head"), P(seq, "head"), P(seq, "head"), P(seq, None), P(seq, None)),
        check_vma=False,
    )
```

```python
import jax
import jax.numpy as jnp
from jax import lax
from jax.sharding import Mesh, PartitionSpec as P

HEADDIM = 64
STATE = 128
BLOCK = 256

F32 = jnp.float32
BF16 = jnp.bfloat16
HIGHEST = lax.Precision.HIGHEST


def rounded(values):
    return values.astype(BF16).astype(F32)


def split_dot(spec, exact, wide, swap=False):
    high = wide.astype(BF16)
    low = (wide - high.astype(F32)).astype(BF16)
    exact = exact.astype(BF16)
    if swap:
        return jnp.einsum(spec, high, exact, preferred_element_type=F32) + jnp.einsum(
            spec, low, exact, preferred_element_type=F32
        )
    return jnp.einsum(spec, exact, high, preferred_element_type=F32) + jnp.einsum(
        spec, exact, low, preferred_element_type=F32
    )


def gather_rows(final, state_grad, total, count):
    heads, width, state = final.shape
    share = heads * width // count
    spare = -(-heads // (8 * state)) * 8
    logs = jnp.pad(total, (0, spare * state - heads)).reshape(spare, state)
    payload = jnp.concatenate(
        [
            final.reshape(count, share, state),
            state_grad.reshape(count, share, state),
            jnp.broadcast_to(logs[None], (count, spare, state)),
        ],
        axis=1,
    )
    return lax.all_to_all(payload, "lo", 0, 0, tiled=True)


def spans_of(mask, logs):
    return jnp.exp(jnp.einsum("...k,kr->...r", mask.astype(F32), logs, precision=HIGHEST))


def scan_rows(got, heads, width, count, split):
    share = heads * width // count
    ends = got[:, :share]
    grads = got[:, share : 2 * share]
    totals = got[:, 2 * share :].reshape(count, -1)[:, :heads]
    place = lax.axis_index("lo")
    row_heads = (place * share + jnp.arange(share)) // width
    logs = jnp.take(totals, row_heads, axis=1)
    order = jnp.arange(count)
    lower = order[None, :] < order[:, None]
    between = lower.T[None, :, :] & lower[:, None, :]
    coef = jnp.where(lower[:, :, None], spans_of(between, logs), 0.0)
    ahead = jnp.sum(coef[:, :, :, None] * ends[None], axis=1)
    behind = jnp.sum(coef[:, :, :, None] * grads[:, None], axis=0)
    if split > 1:
        from_start = spans_of(lower, logs)[:, :, None]
        to_end = spans_of(lower.T, logs)[:, :, None]
        end_state = jnp.sum(to_end * ends, axis=0)
        start_grad = jnp.sum(from_start * grads, axis=0)
        side = lax.axis_index("hi")
        sent = jnp.where(side == 0, end_state, start_grad)
        got_side = lax.ppermute(sent, "hi", [(0, 1), (1, 0)])[None]
        ahead = ahead + jnp.where(side == 1, from_start * got_side, 0.0)
        behind = behind + jnp.where(side == 0, to_end * got_side, 0.0)
    return jnp.concatenate([ahead, behind], axis=1)


def send_back(rows, heads, width, count):
    share = heads * width // count
    back = lax.all_to_all(rows, "lo", 0, 0, tiled=True)
    incoming = back[:, :share].reshape(heads, width, STATE)
    adjoint = back[:, share:].reshape(heads, width, STATE)
    return incoming, adjoint


def head_sum(parts, size):
    if size & (size - 1):
        return lax.psum(parts, "head")
    step = 1
    while step < size:
        pairs = [(i, i ^ step) for i in range(size)]
        parts = jax.tree.map(lambda a: a + lax.ppermute(a, "head", pairs), parts)
        step *= 2
    return parts


def shards(inputs, log_decay, b_proj, c_proj, grad_out, count, head_size, split):
    tokens, head_count = log_decay.shape
    blocks = tokens // BLOCK
    x16 = inputs.reshape(blocks, BLOCK, head_count, HEADDIM).transpose(2, 0, 1, 3)
    g16 = grad_out.reshape(blocks, BLOCK, head_count, HEADDIM).transpose(2, 0, 1, 3)
    xf = x16.astype(F32)
    gf = g16.astype(F32)
    decay = log_decay.reshape(blocks, BLOCK, head_count).transpose(2, 0, 1)
    b16 = b_proj.reshape(blocks, BLOCK, STATE)
    c16 = c_proj.reshape(blocks, BLOCK, STATE)
    bf = b16.astype(F32)
    cf = c16.astype(F32)

    prefix = jnp.cumsum(decay, axis=-1)
    totals = prefix[..., -1]
    causal = jnp.tril(jnp.ones((BLOCK, BLOCK), dtype=bool))
    scores = jnp.einsum("ktn,ksn->kts", c16, b16, preferred_element_type=F32)
    spread = prefix[..., :, None] - prefix[..., None, :]
    decay_mat = jnp.where(causal, jnp.exp(jnp.where(causal, spread, 0.0)), 0.0)
    last_w = jnp.exp(totals[..., None] - prefix)
    scaled = (xf * last_w[..., None]).astype(BF16)
    states = jnp.einsum("hksp,ksn->hkpn", scaled, b16, preferred_element_type=F32)

    gain = jnp.exp(totals)
    local = jnp.zeros(states.shape[:1] + states.shape[2:], F32)
    before = []
    run_log = jnp.zeros((head_count,), F32)
    for k in range(blocks):
        before.append(run_log)
        local = gain[:, k, None, None] * local + states[:, k]
        run_log = run_log + totals[:, k]
    device_total = run_log

    e_prefix = jnp.exp(prefix)
    g_scaled = gf * e_prefix[..., None]
    start_grad = split_dot("hktp,ktn->hkpn", c16, g_scaled, swap=True)
    state_grad = start_grad[:, 0]
    for k in range(1, blocks):
        state_grad = state_grad + jnp.exp(before[k])[:, None, None] * start_grad[:, k]

    if count > 1:
        got = gather_rows(local, state_grad, device_total, count)

    weighted_f = scores[None] * decay_mat
    weighted = weighted_f.astype(BF16)
    within = jnp.einsum("hkts,hksp->hktp", weighted, x16, preferred_element_type=F32)
    d_weighted = jnp.einsum("hktp,hksp->hkts", g16, x16, preferred_element_type=F32)
    d_weighted = rounded(d_weighted)
    d_x_within = rounded(jnp.einsum("hkts,hktp->hksp", weighted, g16, preferred_element_type=F32))
    spread_grad = d_weighted * weighted_f
    d_prefix_within = jnp.sum(spread_grad, axis=-1) - jnp.sum(spread_grad, axis=-2)
    d_scores = jnp.sum(d_weighted * decay_mat, axis=0).astype(BF16)
    d_c_scores = jnp.einsum("kts,ksn->ktn", d_scores, b16, preferred_element_type=F32)
    d_b_scores = jnp.einsum("kts,ktn->ksn", d_scores, c16, preferred_element_type=F32)

    if count > 1:
        got, within, d_x_within, d_prefix_within, d_c_scores, d_b_scores = lax.optimization_barrier(
            (got, within, d_x_within, d_prefix_within, d_c_scores, d_b_scores)
        )
        rows = scan_rows(got, head_count, HEADDIM, count, split)
        incoming, adjoint = send_back(rows, head_count, HEADDIM, count)
    else:
        incoming = jnp.zeros_like(local)
        adjoint = jnp.zeros_like(local)

    starts = [incoming]
    for k in range(blocks - 1):
        starts.append(gain[:, k, None, None] * starts[-1] + states[:, k])
    start = jnp.stack(starts, axis=1)
    carried = split_dot("ktn,hkpn->hktp", c16, start)
    out = within + e_prefix[..., None] * carried
    outputs = out.transpose(1, 2, 0, 3).reshape(tokens, head_count * HEADDIM).astype(BF16)

    d_prefix = jnp.sum(g_scaled * carried, axis=-1) + d_prefix_within
    d_c = jnp.einsum("hktp,hkpn->ktn", g_scaled, start, precision=lax.Precision.HIGH) + d_c_scores

    lam = adjoint
    d_states = [None] * blocks
    d_totals = [None] * blocks
    for k in reversed(range(blocks)):
        d_states[k] = lam
        d_totals[k] = gain[:, k] * jnp.sum(lam * start[:, k], axis=(1, 2))
        lam = start_grad[:, k] + gain[:, k, None, None] * lam
    d_states = jnp.stack(d_states, axis=1)
    d_totals = jnp.stack(d_totals, axis=1)

    d_scaled = rounded(split_dot("ksn,hkpn->hksp", b16, d_states))
    d_b = split_dot("hksp,hkpn->ksn", scaled, d_states) + d_b_scores
    d_x = d_scaled * last_w[..., None] + d_x_within
    d_last = jnp.sum(d_scaled * xf, axis=-1) * last_w
    d_prefix = d_prefix - d_last
    d_totals = d_totals + jnp.sum(d_last, axis=-1)

    d_prefix = d_prefix.at[..., -1].add(d_totals)
    d_decay = lax.cumsum(d_prefix, axis=2, reverse=True)
    grad_decay = d_decay.transpose(1, 2, 0).reshape(tokens, head_count)
    grad_inputs = d_x.transpose(1, 2, 0, 3).reshape(tokens, head_count * HEADDIM).astype(BF16)
    grad_b, grad_c = head_sum((d_b.reshape(tokens, STATE), d_c.reshape(tokens, STATE)), head_size)
    return (outputs, grad_inputs, grad_decay, grad_b, grad_c)


def solution(mesh):
    seq_size = mesh.shape["seq"]
    head_size = mesh.shape["head"]
    split = 2 if seq_size % 4 == 0 else 1
    count = seq_size // split
    grid = Mesh(mesh.devices.reshape(split, count, head_size), ("hi", "lo", "head"))
    seq = ("hi", "lo")
    placed = (P(seq, "head"), P(seq, "head"), P(seq, None), P(seq, None), P(seq, "head"))

    def body(inputs, log_decay, b_proj, c_proj, grad_out):
        return shards(inputs, log_decay, b_proj, c_proj, grad_out, count, head_size, split)

    return jax.shard_map(
        body,
        mesh=grid,
        in_specs=placed,
        out_specs=(P(seq, "head"), P(seq, "head"), P(seq, "head"), P(seq, None), P(seq, None)),
        check_vma=False,
    )
```

```python
import jax
import jax.numpy as jnp
from jax import lax
from jax.sharding import Mesh, PartitionSpec as P

HEADDIM = 64
STATE = 128
BLOCK = 256

F32 = jnp.float32
BF16 = jnp.bfloat16
HIGHEST = lax.Precision.HIGHEST


def rounded(values):
    return values.astype(BF16).astype(F32)


def split_dot(spec, exact, wide, swap=False):
    high = wide.astype(BF16)
    low = (wide - high.astype(F32)).astype(BF16)
    exact = exact.astype(BF16)
    if swap:
        return jnp.einsum(spec, high, exact, preferred_element_type=F32) + jnp.einsum(
            spec, low, exact, preferred_element_type=F32
        )
    return jnp.einsum(spec, exact, high, preferred_element_type=F32) + jnp.einsum(
        spec, exact, low, preferred_element_type=F32
    )


def gather_rows(final, state_grad, total, count):
    heads, width, state = final.shape
    share = heads * width // count
    spare = -(-heads // (8 * state)) * 8
    logs = jnp.pad(total, (0, spare * state - heads)).reshape(spare, state)
    payload = jnp.concatenate(
        [
            final.reshape(count, share, state),
            state_grad.reshape(count, share, state),
            jnp.broadcast_to(logs[None], (count, spare, state)),
        ],
        axis=1,
    )
    return lax.all_to_all(payload, "lo", 0, 0, tiled=True)


def spans_of(mask, logs):
    return jnp.exp(jnp.einsum("...k,kr->...r", mask.astype(F32), logs, precision=HIGHEST))


def scan_rows(got, heads, width, count, split):
    share = heads * width // count
    ends = got[:, :share]
    grads = got[:, share : 2 * share]
    totals = got[:, 2 * share :].reshape(count, -1)[:, :heads]
    place = lax.axis_index("lo")
    row_heads = (place * share + jnp.arange(share)) // width
    logs = jnp.take(totals, row_heads, axis=1)
    order = jnp.arange(count)
    lower = order[None, :] < order[:, None]
    between = lower.T[None, :, :] & lower[:, None, :]
    coef = jnp.where(lower[:, :, None], spans_of(between, logs), 0.0)
    ahead = jnp.sum(coef[:, :, :, None] * ends[None], axis=1)
    behind = jnp.sum(coef[:, :, :, None] * grads[:, None], axis=0)
    if split > 1:
        from_start = spans_of(lower, logs)[:, :, None]
        to_end = spans_of(lower.T, logs)[:, :, None]
        end_state = jnp.sum(to_end * ends, axis=0)
        start_grad = jnp.sum(from_start * grads, axis=0)
        side = lax.axis_index("hi")
        sent = jnp.where(side == 0, end_state, start_grad)
        got_side = lax.ppermute(sent, "hi", [(0, 1), (1, 0)])[None]
        ahead = ahead + jnp.where(side == 1, from_start * got_side, 0.0)
        behind = behind + jnp.where(side == 0, to_end * got_side, 0.0)
    return jnp.concatenate([ahead, behind], axis=1)


def send_back(rows, heads, width, count):
    share = heads * width // count
    incoming = lax.all_to_all(rows[:, :share], "lo", 0, 0, tiled=True)
    adjoint = lax.all_to_all(rows[:, share:], "lo", 0, 0, tiled=True)
    return incoming.reshape(heads, width, STATE), adjoint.reshape(heads, width, STATE)


def head_sum(parts, size):
    if size & (size - 1):
        return lax.psum(parts, "head")
    step = 1
    while step < size:
        pairs = [(i, i ^ step) for i in range(size)]
        parts = jax.tree.map(lambda a: a + lax.ppermute(a, "head", pairs), parts)
        step *= 2
    return parts


def shards(inputs, log_decay, b_proj, c_proj, grad_out, count, head_size, split):
    tokens, head_count = log_decay.shape
    blocks = tokens // BLOCK
    x16 = inputs.reshape(blocks, BLOCK, head_count, HEADDIM).transpose(2, 0, 1, 3)
    g16 = grad_out.reshape(blocks, BLOCK, head_count, HEADDIM).transpose(2, 0, 1, 3)
    xf = x16.astype(F32)
    gf = g16.astype(F32)
    decay = log_decay.reshape(blocks, BLOCK, head_count).transpose(2, 0, 1)
    b16 = b_proj.reshape(blocks, BLOCK, STATE)
    c16 = c_proj.reshape(blocks, BLOCK, STATE)
    bf = b16.astype(F32)
    cf = c16.astype(F32)

    prefix = jnp.cumsum(decay, axis=-1)
    totals = prefix[..., -1]
    causal = jnp.tril(jnp.ones((BLOCK, BLOCK), dtype=bool))
    scores = jnp.einsum("ktn,ksn->kts", c16, b16, preferred_element_type=F32)
    spread = prefix[..., :, None] - prefix[..., None, :]
    decay_mat = jnp.where(causal, jnp.exp(jnp.where(causal, spread, 0.0)), 0.0)
    last_w = jnp.exp(totals[..., None] - prefix)
    scaled = (xf * last_w[..., None]).astype(BF16)
    states = jnp.einsum("hksp,ksn->hkpn", scaled, b16, preferred_element_type=F32)

    gain = jnp.exp(totals)
    local = jnp.zeros(states.shape[:1] + states.shape[2:], F32)
    before = []
    run_log = jnp.zeros((head_count,), F32)
    for k in range(blocks):
        before.append(run_log)
        local = gain[:, k, None, None] * local + states[:, k]
        run_log = run_log + totals[:, k]
    device_total = run_log

    e_prefix = jnp.exp(prefix)
    g_scaled = gf * e_prefix[..., None]
    start_grad = split_dot("hktp,ktn->hkpn", c16, g_scaled, swap=True)
    state_grad = start_grad[:, 0]
    for k in range(1, blocks):
        state_grad = state_grad + jnp.exp(before[k])[:, None, None] * start_grad[:, k]

    if count > 1:
        got = gather_rows(local, state_grad, device_total, count)

    weighted_f = scores[None] * decay_mat
    weighted = weighted_f.astype(BF16)
    within = jnp.einsum("hkts,hksp->hktp", weighted, x16, preferred_element_type=F32)
    d_weighted = jnp.einsum("hktp,hksp->hkts", g16, x16, preferred_element_type=F32)
    d_weighted = rounded(d_weighted)
    d_x_within = rounded(jnp.einsum("hkts,hktp->hksp", weighted, g16, preferred_element_type=F32))
    spread_grad = d_weighted * weighted_f
    d_prefix_within = jnp.sum(spread_grad, axis=-1) - jnp.sum(spread_grad, axis=-2)
    d_scores = jnp.sum(d_weighted * decay_mat, axis=0).astype(BF16)
    d_c_scores = jnp.einsum("kts,ksn->ktn", d_scores, b16, preferred_element_type=F32)
    d_b_scores = jnp.einsum("kts,ktn->ksn", d_scores, c16, preferred_element_type=F32)

    if count > 1:
        got, within, d_x_within, d_prefix_within, d_c_scores, d_b_scores = lax.optimization_barrier(
            (got, within, d_x_within, d_prefix_within, d_c_scores, d_b_scores)
        )
        rows = scan_rows(got, head_count, HEADDIM, count, split)
        incoming, adjoint = send_back(rows, head_count, HEADDIM, count)
    else:
        incoming = jnp.zeros_like(local)
        adjoint = jnp.zeros_like(local)

    starts = [incoming]
    for k in range(blocks - 1):
        starts.append(gain[:, k, None, None] * starts[-1] + states[:, k])
    start = jnp.stack(starts, axis=1)
    carried = split_dot("ktn,hkpn->hktp", c16, start)
    out = within + e_prefix[..., None] * carried
    outputs = out.transpose(1, 2, 0, 3).reshape(tokens, head_count * HEADDIM).astype(BF16)

    d_prefix = jnp.sum(g_scaled * carried, axis=-1) + d_prefix_within
    d_c = jnp.einsum("hktp,hkpn->ktn", g_scaled, start, precision=lax.Precision.HIGH) + d_c_scores

    lam = adjoint
    d_states = [None] * blocks
    d_totals = [None] * blocks
    for k in reversed(range(blocks)):
        d_states[k] = lam
        d_totals[k] = gain[:, k] * jnp.sum(lam * start[:, k], axis=(1, 2))
        lam = start_grad[:, k] + gain[:, k, None, None] * lam
    d_states = jnp.stack(d_states, axis=1)
    d_totals = jnp.stack(d_totals, axis=1)

    d_scaled = rounded(split_dot("ksn,hkpn->hksp", b16, d_states))
    d_b = split_dot("hksp,hkpn->ksn", scaled, d_states) + d_b_scores
    d_x = d_scaled * last_w[..., None] + d_x_within
    d_last = jnp.sum(d_scaled * xf, axis=-1) * last_w
    d_prefix = d_prefix - d_last
    d_totals = d_totals + jnp.sum(d_last, axis=-1)

    d_prefix = d_prefix.at[..., -1].add(d_totals)
    d_decay = lax.cumsum(d_prefix, axis=2, reverse=True)
    grad_decay = d_decay.transpose(1, 2, 0).reshape(tokens, head_count)
    grad_inputs = d_x.transpose(1, 2, 0, 3).reshape(tokens, head_count * HEADDIM).astype(BF16)
    grad_b, grad_c = head_sum((d_b.reshape(tokens, STATE), d_c.reshape(tokens, STATE)), head_size)
    return (outputs, grad_inputs, grad_decay, grad_b, grad_c)


def solution(mesh):
    seq_size = mesh.shape["seq"]
    head_size = mesh.shape["head"]
    split = 2 if seq_size % 4 == 0 else 1
    count = seq_size // split
    grid = Mesh(mesh.devices.reshape(split, count, head_size), ("hi", "lo", "head"))
    seq = ("hi", "lo")
    placed = (P(seq, "head"), P(seq, "head"), P(seq, None), P(seq, None), P(seq, "head"))

    def body(inputs, log_decay, b_proj, c_proj, grad_out):
        return shards(inputs, log_decay, b_proj, c_proj, grad_out, count, head_size, split)

    return jax.shard_map(
        body,
        mesh=grid,
        in_specs=placed,
        out_specs=(P(seq, "head"), P(seq, "head"), P(seq, "head"), P(seq, None), P(seq, None)),
        check_vma=False,
    )
```

```python
import jax
import jax.numpy as jnp
from jax import lax
from jax.sharding import Mesh, PartitionSpec as P

HEADDIM = 64
STATE = 128
BLOCK = 256

F32 = jnp.float32
BF16 = jnp.bfloat16
HIGHEST = lax.Precision.HIGHEST


def rounded(values):
    return values.astype(BF16).astype(F32)


def split_dot(spec, exact, wide, swap=False):
    exact = exact.astype(F32)
    if swap:
        return jnp.einsum(spec, wide, exact, precision=lax.Precision.HIGH)
    return jnp.einsum(spec, exact, wide, precision=lax.Precision.HIGH)


def gather_rows(final, state_grad, total, count):
    heads, width, state = final.shape
    share = heads * width // count
    spare = -(-heads // (8 * state)) * 8
    logs = jnp.pad(total, (0, spare * state - heads)).reshape(spare, state)
    payload = jnp.concatenate(
        [
            final.reshape(count, share, state),
            state_grad.reshape(count, share, state),
            jnp.broadcast_to(logs[None], (count, spare, state)),
        ],
        axis=1,
    )
    return lax.all_to_all(payload, "lo", 0, 0, tiled=True)


def spans_of(mask, logs):
    return jnp.exp(jnp.einsum("...k,kr->...r", mask.astype(F32), logs, precision=HIGHEST))


def scan_rows(got, heads, width, count, split):
    share = heads * width // count
    ends = got[:, :share]
    grads = got[:, share : 2 * share]
    totals = got[:, 2 * share :].reshape(count, -1)[:, :heads]
    place = lax.axis_index("lo")
    row_heads = (place * share + jnp.arange(share)) // width
    logs = jnp.take(totals, row_heads, axis=1)
    order = jnp.arange(count)
    lower = order[None, :] < order[:, None]
    between = lower.T[None, :, :] & lower[:, None, :]
    coef = jnp.where(lower[:, :, None], spans_of(between, logs), 0.0)
    ahead = jnp.sum(coef[:, :, :, None] * ends[None], axis=1)
    behind = jnp.sum(coef[:, :, :, None] * grads[:, None], axis=0)
    if split > 1:
        from_start = spans_of(lower, logs)[:, :, None]
        to_end = spans_of(lower.T, logs)[:, :, None]
        end_state = jnp.sum(to_end * ends, axis=0)
        start_grad = jnp.sum(from_start * grads, axis=0)
        side = lax.axis_index("hi")
        sent = jnp.where(side == 0, end_state, start_grad)
        got_side = lax.ppermute(sent, "hi", [(0, 1), (1, 0)])[None]
        ahead = ahead + jnp.where(side == 1, from_start * got_side, 0.0)
        behind = behind + jnp.where(side == 0, to_end * got_side, 0.0)
    return jnp.concatenate([ahead, behind], axis=1)


def send_back(rows, heads, width, count):
    share = heads * width // count
    incoming = lax.all_to_all(rows[:, :share], "lo", 0, 0, tiled=True)
    adjoint = lax.all_to_all(rows[:, share:], "lo", 0, 0, tiled=True)
    return incoming.reshape(heads, width, STATE), adjoint.reshape(heads, width, STATE)


def head_sum(parts, size):
    if size & (size - 1):
        return lax.psum(parts, "head")
    step = 1
    while step < size:
        pairs = [(i, i ^ step) for i in range(size)]
        parts = jax.tree.map(lambda a: a + lax.ppermute(a, "head", pairs), parts)
        step *= 2
    return parts


def shards(inputs, log_decay, b_proj, c_proj, grad_out, count, head_size, split):
    tokens, head_count = log_decay.shape
    blocks = tokens // BLOCK
    x16 = inputs.reshape(blocks, BLOCK, head_count, HEADDIM).transpose(2, 0, 1, 3)
    g16 = grad_out.reshape(blocks, BLOCK, head_count, HEADDIM).transpose(2, 0, 1, 3)
    xf = x16.astype(F32)
    gf = g16.astype(F32)
    decay = log_decay.reshape(blocks, BLOCK, head_count).transpose(2, 0, 1)
    b16 = b_proj.reshape(blocks, BLOCK, STATE)
    c16 = c_proj.reshape(blocks, BLOCK, STATE)
    bf = b16.astype(F32)
    cf = c16.astype(F32)

    prefix = jnp.cumsum(decay, axis=-1)
    totals = prefix[..., -1]
    causal = jnp.tril(jnp.ones((BLOCK, BLOCK), dtype=bool))
    scores = jnp.einsum("ktn,ksn->kts", c16, b16, preferred_element_type=F32)
    spread = prefix[..., :, None] - prefix[..., None, :]
    decay_mat = jnp.where(causal, jnp.exp(jnp.where(causal, spread, 0.0)), 0.0)
    last_w = jnp.exp(totals[..., None] - prefix)
    scaled = (xf * last_w[..., None]).astype(BF16)
    states = jnp.einsum("hksp,ksn->hkpn", scaled, b16, preferred_element_type=F32)

    gain = jnp.exp(totals)
    local = jnp.zeros(states.shape[:1] + states.shape[2:], F32)
    before = []
    run_log = jnp.zeros((head_count,), F32)
    for k in range(blocks):
        before.append(run_log)
        local = gain[:, k, None, None] * local + states[:, k]
        run_log = run_log + totals[:, k]
    device_total = run_log

    e_prefix = jnp.exp(prefix)
    g_scaled = gf * e_prefix[..., None]
    start_grad = split_dot("hktp,ktn->hkpn", c16, g_scaled, swap=True)
    state_grad = start_grad[:, 0]
    for k in range(1, blocks):
        state_grad = state_grad + jnp.exp(before[k])[:, None, None] * start_grad[:, k]

    if count > 1:
        got = gather_rows(local, state_grad, device_total, count)

    weighted_f = scores[None] * decay_mat
    weighted = weighted_f.astype(BF16)
    within = jnp.einsum("hkts,hksp->hktp", weighted, x16, preferred_element_type=F32)
    d_weighted = jnp.einsum("hktp,hksp->hkts", g16, x16, preferred_element_type=F32)
    d_weighted = rounded(d_weighted)
    d_x_within = rounded(jnp.einsum("hkts,hktp->hksp", weighted, g16, preferred_element_type=F32))
    spread_grad = d_weighted * weighted_f
    d_prefix_within = jnp.sum(spread_grad, axis=-1) - jnp.sum(spread_grad, axis=-2)
    d_scores = jnp.sum(d_weighted * decay_mat, axis=0).astype(BF16)
    d_c_scores = jnp.einsum("kts,ksn->ktn", d_scores, b16, preferred_element_type=F32)
    d_b_scores = jnp.einsum("kts,ktn->ksn", d_scores, c16, preferred_element_type=F32)

    if count > 1:
        got, within, d_x_within, d_prefix_within, d_c_scores, d_b_scores = lax.optimization_barrier(
            (got, within, d_x_within, d_prefix_within, d_c_scores, d_b_scores)
        )
        rows = scan_rows(got, head_count, HEADDIM, count, split)
        incoming, adjoint = send_back(rows, head_count, HEADDIM, count)
    else:
        incoming = jnp.zeros_like(local)
        adjoint = jnp.zeros_like(local)

    starts = [incoming]
    for k in range(blocks - 1):
        starts.append(gain[:, k, None, None] * starts[-1] + states[:, k])
    start = jnp.stack(starts, axis=1)
    carried = split_dot("ktn,hkpn->hktp", c16, start)
    out = within + e_prefix[..., None] * carried
    outputs = out.transpose(1, 2, 0, 3).reshape(tokens, head_count * HEADDIM).astype(BF16)

    d_prefix = jnp.sum(g_scaled * carried, axis=-1) + d_prefix_within
    d_c = jnp.einsum("hktp,hkpn->ktn", g_scaled, start, precision=lax.Precision.HIGH) + d_c_scores

    lam = adjoint
    d_states = [None] * blocks
    d_totals = [None] * blocks
    for k in reversed(range(blocks)):
        d_states[k] = lam
        d_totals[k] = gain[:, k] * jnp.sum(lam * start[:, k], axis=(1, 2))
        lam = start_grad[:, k] + gain[:, k, None, None] * lam
    d_states = jnp.stack(d_states, axis=1)
    d_totals = jnp.stack(d_totals, axis=1)

    d_scaled = rounded(split_dot("ksn,hkpn->hksp", b16, d_states))
    d_b = split_dot("hksp,hkpn->ksn", scaled, d_states) + d_b_scores
    d_x = d_scaled * last_w[..., None] + d_x_within
    d_last = jnp.sum(d_scaled * xf, axis=-1) * last_w
    d_prefix = d_prefix - d_last
    d_totals = d_totals + jnp.sum(d_last, axis=-1)

    d_prefix = d_prefix.at[..., -1].add(d_totals)
    d_decay = lax.cumsum(d_prefix, axis=2, reverse=True)
    grad_decay = d_decay.transpose(1, 2, 0).reshape(tokens, head_count)
    grad_inputs = d_x.transpose(1, 2, 0, 3).reshape(tokens, head_count * HEADDIM).astype(BF16)
    grad_b, grad_c = head_sum((d_b.reshape(tokens, STATE), d_c.reshape(tokens, STATE)), head_size)
    return (outputs, grad_inputs, grad_decay, grad_b, grad_c)


def solution(mesh):
    seq_size = mesh.shape["seq"]
    head_size = mesh.shape["head"]
    split = 2 if seq_size % 4 == 0 else 1
    count = seq_size // split
    grid = Mesh(mesh.devices.reshape(split, count, head_size), ("hi", "lo", "head"))
    seq = ("hi", "lo")
    placed = (P(seq, "head"), P(seq, "head"), P(seq, None), P(seq, None), P(seq, "head"))

    def body(inputs, log_decay, b_proj, c_proj, grad_out):
        return shards(inputs, log_decay, b_proj, c_proj, grad_out, count, head_size, split)

    return jax.shard_map(
        body,
        mesh=grid,
        in_specs=placed,
        out_specs=(P(seq, "head"), P(seq, "head"), P(seq, "head"), P(seq, None), P(seq, None)),
        check_vma=False,
    )
```

```python
import jax
import jax.numpy as jnp
from jax import lax
from jax.sharding import Mesh, PartitionSpec as P

HEADDIM = 64
STATE = 128
BLOCK = 256

F32 = jnp.float32
BF16 = jnp.bfloat16
HIGHEST = lax.Precision.HIGHEST


def rounded(values):
    return values.astype(BF16).astype(F32)


def split_dot(spec, exact, wide, swap=False):
    high = wide.astype(BF16)
    low = (wide - high.astype(F32)).astype(BF16)
    exact = exact.astype(BF16)
    if swap:
        return jnp.einsum(spec, high, exact, preferred_element_type=F32) + jnp.einsum(
            spec, low, exact, preferred_element_type=F32
        )
    return jnp.einsum(spec, exact, high, preferred_element_type=F32) + jnp.einsum(
        spec, exact, low, preferred_element_type=F32
    )


def gather_rows(final, state_grad, total, count):
    heads, width, state = final.shape
    share = heads * width // count
    spare = -(-heads // (8 * state)) * 8
    logs = jnp.pad(total, (0, spare * state - heads)).reshape(spare, state)
    payload = jnp.concatenate(
        [
            final.reshape(count, share, state),
            state_grad.reshape(count, share, state),
            jnp.broadcast_to(logs[None], (count, spare, state)),
        ],
        axis=1,
    )
    return lax.all_to_all(payload, "lo", 0, 0, tiled=True)


def spans_of(mask, logs):
    return jnp.exp(jnp.einsum("...k,kr->...r", mask.astype(F32), logs, precision=HIGHEST))


def scan_rows(got, heads, width, count, split):
    share = heads * width // count
    ends = got[:, :share]
    grads = got[:, share : 2 * share]
    totals = got[:, 2 * share :].reshape(count, -1)[:, :heads]
    place = lax.axis_index("lo")
    row_heads = (place * share + jnp.arange(share)) // width
    logs = jnp.take(totals, row_heads, axis=1)
    order = jnp.arange(count)
    lower = order[None, :] < order[:, None]
    between = lower.T[None, :, :] & lower[:, None, :]
    coef = jnp.where(lower[:, :, None], spans_of(between, logs), 0.0)
    ahead = jnp.sum(coef[:, :, :, None] * ends[None], axis=1)
    behind = jnp.sum(coef[:, :, :, None] * grads[:, None], axis=0)
    if split > 1:
        from_start = spans_of(lower, logs)[:, :, None]
        to_end = spans_of(lower.T, logs)[:, :, None]
        end_state = jnp.sum(to_end * ends, axis=0)
        start_grad = jnp.sum(from_start * grads, axis=0)
        side = lax.axis_index("hi")
        sent = jnp.where(side == 0, end_state, start_grad)
        got_side = lax.ppermute(sent, "hi", [(0, 1), (1, 0)])[None]
        ahead = ahead + jnp.where(side == 1, from_start * got_side, 0.0)
        behind = behind + jnp.where(side == 0, to_end * got_side, 0.0)
    return jnp.concatenate([ahead, behind], axis=1)


def send_back(rows, heads, width, count):
    share = heads * width // count
    incoming = lax.all_to_all(rows[:, :share], "lo", 0, 0, tiled=True)
    adjoint = lax.all_to_all(rows[:, share:], "lo", 0, 0, tiled=True)
    return incoming.reshape(heads, width, STATE), adjoint.reshape(heads, width, STATE)


def head_sum(parts, size):
    if size & (size - 1):
        return lax.psum(parts, "head")
    step = 1
    while step < size:
        pairs = [(i, i ^ step) for i in range(size)]
        parts = jax.tree.map(lambda a: a + lax.ppermute(a, "head", pairs), parts)
        step *= 2
    return parts


def shards(inputs, log_decay, b_proj, c_proj, grad_out, count, head_size, split):
    tokens, head_count = log_decay.shape
    blocks = tokens // BLOCK
    xr = inputs.reshape(blocks, BLOCK, head_count, HEADDIM)
    gr = grad_out.reshape(blocks, BLOCK, head_count, HEADDIM)
    xrf = xr.astype(F32)
    grf = gr.astype(F32)
    decay = log_decay.reshape(blocks, BLOCK, head_count)
    b16 = b_proj.reshape(blocks, BLOCK, STATE)
    c16 = c_proj.reshape(blocks, BLOCK, STATE)

    prefix = jnp.cumsum(decay, axis=1)
    totals = prefix[:, -1, :]
    last_w = jnp.exp(totals[:, None, :] - prefix)
    scaled = (xrf * last_w[..., None]).astype(BF16)
    states = jnp.einsum("kshp,ksn->khpn", scaled, b16, preferred_element_type=F32)
    gain = jnp.exp(totals)
    local = jnp.zeros(states.shape[1:], F32)
    before = []
    run_log = jnp.zeros((head_count,), F32)
    for k in range(blocks):
        before.append(run_log)
        local = gain[k][:, None, None] * local + states[k]
        run_log = run_log + totals[k]
    device_total = run_log

    e_prefix = jnp.exp(prefix)
    g_scaled = grf * e_prefix[..., None]
    start_grad = split_dot("kthp,ktn->khpn", c16, g_scaled, swap=True)
    state_grad = start_grad[0]
    for k in range(1, blocks):
        state_grad = state_grad + jnp.exp(before[k])[:, None, None] * start_grad[k]

    if count > 1:
        got = gather_rows(local, state_grad, device_total, count)

    x16 = xr.transpose(2, 0, 1, 3)
    g16 = gr.transpose(2, 0, 1, 3)
    prefix_h = prefix.transpose(2, 0, 1)
    causal = jnp.tril(jnp.ones((BLOCK, BLOCK), dtype=bool))
    scores = jnp.einsum("ktn,ksn->kts", c16, b16, preferred_element_type=F32)
    spread = prefix_h[..., :, None] - prefix_h[..., None, :]
    decay_mat = jnp.where(causal, jnp.exp(jnp.where(causal, spread, 0.0)), 0.0)
    weighted_f = scores[None] * decay_mat
    weighted = weighted_f.astype(BF16)
    within = jnp.einsum("hkts,hksp->hktp", weighted, x16, preferred_element_type=F32)
    within = within.transpose(1, 2, 0, 3)
    d_weighted = jnp.einsum("hktp,hksp->hkts", g16, x16, preferred_element_type=F32)
    d_weighted = rounded(d_weighted)
    d_x_within = rounded(jnp.einsum("hkts,hktp->hksp", weighted, g16, preferred_element_type=F32))
    d_x_within = d_x_within.transpose(1, 2, 0, 3)
    spread_grad = d_weighted * weighted_f
    d_prefix_within = jnp.sum(spread_grad, axis=-1) - jnp.sum(spread_grad, axis=-2)
    d_prefix_within = d_prefix_within.transpose(1, 2, 0)
    d_scores = jnp.sum(d_weighted * decay_mat, axis=0).astype(BF16)
    d_c_scores = jnp.einsum("kts,ksn->ktn", d_scores, b16, preferred_element_type=F32)
    d_b_scores = jnp.einsum("kts,ktn->ksn", d_scores, c16, preferred_element_type=F32)

    if count > 1:
        got, within, d_x_within, d_prefix_within, d_c_scores, d_b_scores = lax.optimization_barrier(
            (got, within, d_x_within, d_prefix_within, d_c_scores, d_b_scores)
        )
        rows = scan_rows(got, head_count, HEADDIM, count, split)
        incoming, adjoint = send_back(rows, head_count, HEADDIM, count)
    else:
        incoming = jnp.zeros_like(local)
        adjoint = jnp.zeros_like(local)

    starts = [incoming]
    for k in range(blocks - 1):
        starts.append(gain[k][:, None, None] * starts[-1] + states[k])
    start = jnp.stack(starts, axis=0)
    carried = split_dot("ktn,khpn->kthp", c16, start)
    out = within + e_prefix[..., None] * carried
    outputs = out.reshape(tokens, head_count * HEADDIM).astype(BF16)

    d_prefix = jnp.sum(g_scaled * carried, axis=-1) + d_prefix_within
    d_c = jnp.einsum("kthp,khpn->ktn", g_scaled, start, precision=lax.Precision.HIGH) + d_c_scores

    lam = adjoint
    d_states = [None] * blocks
    d_totals = [None] * blocks
    for k in reversed(range(blocks)):
        d_states[k] = lam
        d_totals[k] = gain[k] * jnp.sum(lam * start[k], axis=(1, 2))
        lam = start_grad[k] + gain[k][:, None, None] * lam
    d_states = jnp.stack(d_states, axis=0)
    d_totals = jnp.stack(d_totals, axis=0)

    d_scaled = rounded(split_dot("ksn,khpn->kshp", b16, d_states))
    d_b = split_dot("kshp,khpn->ksn", scaled, d_states) + d_b_scores
    d_x = d_scaled * last_w[..., None] + d_x_within
    d_last = jnp.sum(d_scaled * xrf, axis=-1) * last_w
    d_prefix = d_prefix - d_last
    d_totals = d_totals + jnp.sum(d_last, axis=1)

    d_prefix = d_prefix.at[:, -1, :].add(d_totals)
    d_decay = lax.cumsum(d_prefix, axis=1, reverse=True)
    grad_decay = d_decay.reshape(tokens, head_count)
    grad_inputs = d_x.reshape(tokens, head_count * HEADDIM).astype(BF16)
    grad_b, grad_c = head_sum((d_b.reshape(tokens, STATE), d_c.reshape(tokens, STATE)), head_size)
    return (outputs, grad_inputs, grad_decay, grad_b, grad_c)


def solution(mesh):
    seq_size = mesh.shape["seq"]
    head_size = mesh.shape["head"]
    split = 2 if seq_size % 4 == 0 else 1
    count = seq_size // split
    grid = Mesh(mesh.devices.reshape(split, count, head_size), ("hi", "lo", "head"))
    seq = ("hi", "lo")
    placed = (P(seq, "head"), P(seq, "head"), P(seq, None), P(seq, None), P(seq, "head"))

    def body(inputs, log_decay, b_proj, c_proj, grad_out):
        return shards(inputs, log_decay, b_proj, c_proj, grad_out, count, head_size, split)

    return jax.shard_map(
        body,
        mesh=grid,
        in_specs=placed,
        out_specs=(P(seq, "head"), P(seq, "head"), P(seq, "head"), P(seq, None), P(seq, None)),
        check_vma=False,
    )
```

```python
import jax
import jax.numpy as jnp
from jax import lax
from jax.sharding import Mesh, PartitionSpec as P

HEADDIM = 64
STATE = 128
BLOCK = 256

F32 = jnp.float32
BF16 = jnp.bfloat16
HIGHEST = lax.Precision.HIGHEST


def rounded(values):
    return values.astype(BF16).astype(F32)


def split_dot(spec, exact, wide, swap=False):
    high = wide.astype(BF16)
    low = (wide - high.astype(F32)).astype(BF16)
    exact = exact.astype(BF16)
    if swap:
        return jnp.einsum(spec, high, exact, preferred_element_type=F32) + jnp.einsum(
            spec, low, exact, preferred_element_type=F32
        )
    return jnp.einsum(spec, exact, high, preferred_element_type=F32) + jnp.einsum(
        spec, exact, low, preferred_element_type=F32
    )


def gather_rows(final, state_grad, total, count):
    heads, width, state = final.shape
    share = heads * width // count
    spare = -(-heads // (8 * state)) * 8
    logs = jnp.pad(total, (0, spare * state - heads)).reshape(spare, state)
    payload = jnp.concatenate(
        [
            final.reshape(count, share, state),
            state_grad.reshape(count, share, state),
            jnp.broadcast_to(logs[None], (count, spare, state)),
        ],
        axis=1,
    )
    return lax.all_to_all(payload, "lo", 0, 0, tiled=True)


def spans_of(mask, logs):
    return jnp.exp(jnp.einsum("...k,kr->...r", mask.astype(F32), logs, precision=HIGHEST))


def scan_rows(got, heads, width, count, split):
    share = heads * width // count
    ends = got[:, :share]
    grads = got[:, share : 2 * share]
    totals = got[:, 2 * share :].reshape(count, -1)[:, :heads]
    place = lax.axis_index("lo")
    row_heads = (place * share + jnp.arange(share)) // width
    logs = jnp.take(totals, row_heads, axis=1)
    order = jnp.arange(count)
    lower = order[None, :] < order[:, None]
    between = lower.T[None, :, :] & lower[:, None, :]
    coef = jnp.where(lower[:, :, None], spans_of(between, logs), 0.0)
    ahead = jnp.sum(coef[:, :, :, None] * ends[None], axis=1)
    behind = jnp.sum(coef[:, :, :, None] * grads[:, None], axis=0)
    if split > 1:
        from_start = spans_of(lower, logs)[:, :, None]
        to_end = spans_of(lower.T, logs)[:, :, None]
        end_state = jnp.sum(to_end * ends, axis=0)
        start_grad = jnp.sum(from_start * grads, axis=0)
        side = lax.axis_index("hi")
        sent = jnp.where(side == 0, end_state, start_grad)
        got_side = lax.ppermute(sent, "hi", [(0, 1), (1, 0)])[None]
        ahead = ahead + jnp.where(side == 1, from_start * got_side, 0.0)
        behind = behind + jnp.where(side == 0, to_end * got_side, 0.0)
    return jnp.concatenate([ahead, behind], axis=1)


def send_back(rows, heads, width, count):
    share = heads * width // count
    incoming = lax.all_to_all(rows[:, :share], "lo", 0, 0, tiled=True)
    adjoint = lax.all_to_all(rows[:, share:], "lo", 0, 0, tiled=True)
    return incoming.reshape(heads, width, STATE), adjoint.reshape(heads, width, STATE)


def head_sum(parts, size):
    if size & (size - 1):
        return lax.psum(parts, "head")
    step = 1
    while step < size:
        pairs = [(i, i ^ step) for i in range(size)]
        parts = jax.tree.map(lambda a: a + lax.ppermute(a, "head", pairs), parts)
        step *= 2
    return parts


def shards(inputs, log_decay, b_proj, c_proj, grad_out, count, head_size, split):
    tokens, head_count = log_decay.shape
    blocks = tokens // BLOCK
    x16 = inputs.reshape(blocks, BLOCK, head_count, HEADDIM).transpose(2, 0, 1, 3)
    g16 = grad_out.reshape(blocks, BLOCK, head_count, HEADDIM).transpose(2, 0, 1, 3)
    xf = x16.astype(F32)
    gf = g16.astype(F32)
    decay = log_decay.reshape(blocks, BLOCK, head_count).transpose(2, 0, 1)
    b16 = b_proj.reshape(blocks, BLOCK, STATE)
    c16 = c_proj.reshape(blocks, BLOCK, STATE)
    bf = b16.astype(F32)
    cf = c16.astype(F32)

    prefix = jnp.cumsum(decay, axis=-1)
    totals = prefix[..., -1]
    causal = jnp.tril(jnp.ones((BLOCK, BLOCK), dtype=bool))
    scores = jnp.einsum("ktn,ksn->kts", c16, b16, preferred_element_type=F32)
    spread = prefix[..., :, None] - prefix[..., None, :]
    decay_mat = jnp.where(causal, jnp.exp(jnp.where(causal, spread, 0.0)), 0.0)
    last_w = jnp.exp(totals[..., None] - prefix)
    scaled = (xf * last_w[..., None]).astype(BF16)
    states = jnp.einsum("hksp,ksn->hkpn", scaled, b16, preferred_element_type=F32)

    gain = jnp.exp(totals)
    local = jnp.zeros(states.shape[:1] + states.shape[2:], F32)
    before = []
    run_log = jnp.zeros((head_count,), F32)
    for k in range(blocks):
        before.append(run_log)
        local = gain[:, k, None, None] * local + states[:, k]
        run_log = run_log + totals[:, k]
    device_total = run_log

    e_prefix = jnp.exp(prefix)
    g_scaled = gf * e_prefix[..., None]
    start_grad = split_dot("hktp,ktn->hkpn", c16, g_scaled, swap=True)
    state_grad = start_grad[:, 0]
    for k in range(1, blocks):
        state_grad = state_grad + jnp.exp(before[k])[:, None, None] * start_grad[:, k]

    if count > 1:
        got = gather_rows(local, state_grad, device_total, count)

    weighted_f = scores[None] * decay_mat
    weighted = weighted_f.astype(BF16)
    within = jnp.einsum("hkts,hksp->hktp", weighted, x16, preferred_element_type=F32)
    d_weighted = jnp.einsum("hktp,hksp->hkts", g16, x16, preferred_element_type=F32)
    d_weighted = rounded(d_weighted)
    d_x_within = rounded(jnp.einsum("hkts,hktp->hksp", weighted, g16, preferred_element_type=F32))
    spread_grad = d_weighted * weighted_f
    d_prefix_within = jnp.sum(spread_grad, axis=-1) - jnp.sum(spread_grad, axis=-2)
    d_scores = jnp.sum(d_weighted * decay_mat, axis=0).astype(BF16)
    d_c_scores = jnp.einsum("kts,ksn->ktn", d_scores, b16, preferred_element_type=F32)
    d_b_scores = jnp.einsum("kts,ktn->ksn", d_scores, c16, preferred_element_type=F32)

    if count > 1:
        got, within, d_x_within, d_prefix_within, d_c_scores, d_b_scores = lax.optimization_barrier(
            (got, within, d_x_within, d_prefix_within, d_c_scores, d_b_scores)
        )
        rows = scan_rows(got, head_count, HEADDIM, count, split)
        incoming, adjoint = send_back(rows, head_count, HEADDIM, count)
    else:
        incoming = jnp.zeros_like(local)
        adjoint = jnp.zeros_like(local)

    starts = [incoming]
    for k in range(blocks - 1):
        starts.append(gain[:, k, None, None] * starts[-1] + states[:, k])
    start = jnp.stack(starts, axis=1)
    carried = split_dot("ktn,hkpn->hktp", c16, start)
    out = within + e_prefix[..., None] * carried
    outputs = out.transpose(1, 2, 0, 3).reshape(tokens, head_count * HEADDIM).astype(BF16)

    d_prefix = jnp.sum(g_scaled * carried, axis=-1) + d_prefix_within
    d_c = jnp.einsum("hktp,hkpn->ktn", g_scaled, start, precision=lax.Precision.HIGH) + d_c_scores

    lam = adjoint
    d_states = [None] * blocks
    d_totals = [None] * blocks
    for k in reversed(range(blocks)):
        d_states[k] = lam
        d_totals[k] = gain[:, k] * jnp.sum(lam * start[:, k], axis=(1, 2))
        lam = start_grad[:, k] + gain[:, k, None, None] * lam
    d_states = jnp.stack(d_states, axis=1)
    d_totals = jnp.stack(d_totals, axis=1)

    d_scaled = rounded(split_dot("ksn,hkpn->hksp", b16, d_states))
    d_b = split_dot("hksp,hkpn->ksn", scaled, d_states) + d_b_scores
    d_x = d_scaled * last_w[..., None] + d_x_within
    d_last = jnp.sum(d_scaled * xf, axis=-1) * last_w
    d_prefix = d_prefix - d_last
    d_totals = d_totals + jnp.sum(d_last, axis=-1)

    d_prefix = d_prefix.at[..., -1].add(d_totals)
    upper = jnp.triu(jnp.ones((BLOCK, BLOCK), F32)).T
    d_decay = jnp.einsum("hkt,ts->hks", d_prefix, upper, precision=HIGHEST)
    grad_decay = d_decay.transpose(1, 2, 0).reshape(tokens, head_count)
    grad_inputs = d_x.transpose(1, 2, 0, 3).reshape(tokens, head_count * HEADDIM).astype(BF16)
    grad_b, grad_c = head_sum((d_b.reshape(tokens, STATE), d_c.reshape(tokens, STATE)), head_size)
    return (outputs, grad_inputs, grad_decay, grad_b, grad_c)


def solution(mesh):
    seq_size = mesh.shape["seq"]
    head_size = mesh.shape["head"]
    split = 2 if seq_size % 4 == 0 else 1
    count = seq_size // split
    grid = Mesh(mesh.devices.reshape(split, count, head_size), ("hi", "lo", "head"))
    seq = ("hi", "lo")
    placed = (P(seq, "head"), P(seq, "head"), P(seq, None), P(seq, None), P(seq, "head"))

    def body(inputs, log_decay, b_proj, c_proj, grad_out):
        return shards(inputs, log_decay, b_proj, c_proj, grad_out, count, head_size, split)

    return jax.shard_map(
        body,
        mesh=grid,
        in_specs=placed,
        out_specs=(P(seq, "head"), P(seq, "head"), P(seq, "head"), P(seq, None), P(seq, None)),
        check_vma=False,
    )
```

```python
import jax
import jax.numpy as jnp
from jax import lax
from jax.sharding import Mesh, PartitionSpec as P

HEADDIM = 64
STATE = 128
BLOCK = 256

F32 = jnp.float32
BF16 = jnp.bfloat16
HIGHEST = lax.Precision.HIGHEST


def rounded(values):
    return values.astype(BF16).astype(F32)


def split_dot(spec, exact, wide, swap=False):
    high = wide.astype(BF16)
    low = (wide - high.astype(F32)).astype(BF16)
    exact = exact.astype(BF16)
    if swap:
        return jnp.einsum(spec, high, exact, preferred_element_type=F32) + jnp.einsum(
            spec, low, exact, preferred_element_type=F32
        )
    return jnp.einsum(spec, exact, high, preferred_element_type=F32) + jnp.einsum(
        spec, exact, low, preferred_element_type=F32
    )


def gather_rows(final, state_grad, total, count):
    heads, width, state = final.shape
    share = heads * width // count
    spare = -(-heads // (8 * state)) * 8
    logs = jnp.pad(total, (0, spare * state - heads)).reshape(spare, state)
    payload = jnp.concatenate(
        [
            final.reshape(count, share, state),
            state_grad.reshape(count, share, state),
            jnp.broadcast_to(logs[None], (count, spare, state)),
        ],
        axis=1,
    )
    return lax.all_to_all(payload, "lo", 0, 0, tiled=True)


def spans_of(mask, logs):
    return jnp.exp(jnp.einsum("...k,kr->...r", mask.astype(F32), logs, precision=HIGHEST))


def scan_rows(got, heads, width, count, split):
    share = heads * width // count
    ends = got[:, :share]
    grads = got[:, share : 2 * share]
    totals = got[:, 2 * share :].reshape(count, -1)[:, :heads]
    place = lax.axis_index("lo")
    if share % width == 0:
        owned = share // width
        logs = lax.dynamic_slice_in_dim(totals, place * owned, owned, axis=1)
        logs = jnp.repeat(logs, width, axis=1)
    else:
        row_heads = (place * share + jnp.arange(share)) // width
        logs = jnp.take(totals, row_heads, axis=1)
    order = jnp.arange(count)
    lower = order[None, :] < order[:, None]
    between = lower.T[None, :, :] & lower[:, None, :]
    coef = jnp.where(lower[:, :, None], spans_of(between, logs), 0.0)
    ahead = jnp.sum(coef[:, :, :, None] * ends[None], axis=1)
    behind = jnp.sum(coef[:, :, :, None] * grads[:, None], axis=0)
    if split > 1:
        from_start = spans_of(lower, logs)[:, :, None]
        to_end = spans_of(lower.T, logs)[:, :, None]
        end_state = jnp.sum(to_end * ends, axis=0)
        start_grad = jnp.sum(from_start * grads, axis=0)
        side = lax.axis_index("hi")
        sent = jnp.where(side == 0, end_state, start_grad)
        got_side = lax.ppermute(sent, "hi", [(0, 1), (1, 0)])[None]
        ahead = ahead + jnp.where(side == 1, from_start * got_side, 0.0)
        behind = behind + jnp.where(side == 0, to_end * got_side, 0.0)
    return jnp.concatenate([ahead, behind], axis=1)


def send_back(rows, heads, width, count):
    share = heads * width // count
    incoming = lax.all_to_all(rows[:, :share], "lo", 0, 0, tiled=True)
    adjoint = lax.all_to_all(rows[:, share:], "lo", 0, 0, tiled=True)
    return incoming.reshape(heads, width, STATE), adjoint.reshape(heads, width, STATE)


def head_sum(parts, size):
    if size & (size - 1):
        return lax.psum(parts, "head")
    step = 1
    while step < size:
        pairs = [(i, i ^ step) for i in range(size)]
        parts = jax.tree.map(lambda a: a + lax.ppermute(a, "head", pairs), parts)
        step *= 2
    return parts


def shards(inputs, log_decay, b_proj, c_proj, grad_out, count, head_size, split):
    tokens, head_count = log_decay.shape
    blocks = tokens // BLOCK
    x16 = inputs.reshape(blocks, BLOCK, head_count, HEADDIM).transpose(2, 0, 1, 3)
    g16 = grad_out.reshape(blocks, BLOCK, head_count, HEADDIM).transpose(2, 0, 1, 3)
    xf = x16.astype(F32)
    gf = g16.astype(F32)
    decay = log_decay.reshape(blocks, BLOCK, head_count).transpose(2, 0, 1)
    b16 = b_proj.reshape(blocks, BLOCK, STATE)
    c16 = c_proj.reshape(blocks, BLOCK, STATE)
    bf = b16.astype(F32)
    cf = c16.astype(F32)

    prefix = jnp.cumsum(decay, axis=-1)
    totals = prefix[..., -1]
    causal = jnp.tril(jnp.ones((BLOCK, BLOCK), dtype=bool))
    scores = jnp.einsum("ktn,ksn->kts", c16, b16, preferred_element_type=F32)
    spread = prefix[..., :, None] - prefix[..., None, :]
    decay_mat = jnp.where(causal, jnp.exp(jnp.where(causal, spread, 0.0)), 0.0)
    last_w = jnp.exp(totals[..., None] - prefix)
    scaled = (xf * last_w[..., None]).astype(BF16)
    states = jnp.einsum("hksp,ksn->hkpn", scaled, b16, preferred_element_type=F32)

    gain = jnp.exp(totals)
    local = jnp.zeros(states.shape[:1] + states.shape[2:], F32)
    before = []
    run_log = jnp.zeros((head_count,), F32)
    for k in range(blocks):
        before.append(run_log)
        local = gain[:, k, None, None] * local + states[:, k]
        run_log = run_log + totals[:, k]
    device_total = run_log

    e_prefix = jnp.exp(prefix)
    g_scaled = gf * e_prefix[..., None]
    start_grad = split_dot("hktp,ktn->hkpn", c16, g_scaled, swap=True)
    state_grad = start_grad[:, 0]
    for k in range(1, blocks):
        state_grad = state_grad + jnp.exp(before[k])[:, None, None] * start_grad[:, k]

    if count > 1:
        got = gather_rows(local, state_grad, device_total, count)

    weighted_f = scores[None] * decay_mat
    weighted = weighted_f.astype(BF16)
    within = jnp.einsum("hkts,hksp->hktp", weighted, x16, preferred_element_type=F32)
    d_weighted = jnp.einsum("hktp,hksp->hkts", g16, x16, preferred_element_type=F32)
    d_weighted = rounded(d_weighted)
    d_x_within = rounded(jnp.einsum("hkts,hktp->hksp", weighted, g16, preferred_element_type=F32))
    spread_grad = d_weighted * weighted_f
    d_prefix_within = jnp.sum(spread_grad, axis=-1) - jnp.sum(spread_grad, axis=-2)
    d_scores = jnp.sum(d_weighted * decay_mat, axis=0).astype(BF16)
    d_c_scores = jnp.einsum("kts,ksn->ktn", d_scores, b16, preferred_element_type=F32)
    d_b_scores = jnp.einsum("kts,ktn->ksn", d_scores, c16, preferred_element_type=F32)

    if count > 1:
        got, within, d_x_within, d_prefix_within, d_c_scores, d_b_scores = lax.optimization_barrier(
            (got, within, d_x_within, d_prefix_within, d_c_scores, d_b_scores)
        )
        rows = scan_rows(got, head_count, HEADDIM, count, split)
        incoming, adjoint = send_back(rows, head_count, HEADDIM, count)
    else:
        incoming = jnp.zeros_like(local)
        adjoint = jnp.zeros_like(local)

    starts = [incoming]
    for k in range(blocks - 1):
        starts.append(gain[:, k, None, None] * starts[-1] + states[:, k])
    start = jnp.stack(starts, axis=1)
    carried = split_dot("ktn,hkpn->hktp", c16, start)
    out = within + e_prefix[..., None] * carried
    outputs = out.transpose(1, 2, 0, 3).reshape(tokens, head_count * HEADDIM).astype(BF16)

    d_prefix = jnp.sum(g_scaled * carried, axis=-1) + d_prefix_within
    d_c = jnp.einsum("hktp,hkpn->ktn", g_scaled, start, precision=lax.Precision.HIGH) + d_c_scores

    lam = adjoint
    d_states = [None] * blocks
    d_totals = [None] * blocks
    for k in reversed(range(blocks)):
        d_states[k] = lam
        d_totals[k] = gain[:, k] * jnp.sum(lam * start[:, k], axis=(1, 2))
        lam = start_grad[:, k] + gain[:, k, None, None] * lam
    d_states = jnp.stack(d_states, axis=1)
    d_totals = jnp.stack(d_totals, axis=1)

    d_scaled = rounded(split_dot("ksn,hkpn->hksp", b16, d_states))
    d_b = split_dot("hksp,hkpn->ksn", scaled, d_states) + d_b_scores
    d_x = d_scaled * last_w[..., None] + d_x_within
    d_last = jnp.sum(d_scaled * xf, axis=-1) * last_w
    d_prefix = d_prefix - d_last
    d_totals = d_totals + jnp.sum(d_last, axis=-1)

    d_prefix = d_prefix.at[..., -1].add(d_totals)
    d_decay = lax.cumsum(d_prefix, axis=2, reverse=True)
    grad_decay = d_decay.transpose(1, 2, 0).reshape(tokens, head_count)
    grad_inputs = d_x.transpose(1, 2, 0, 3).reshape(tokens, head_count * HEADDIM).astype(BF16)
    grad_b, grad_c = head_sum((d_b.reshape(tokens, STATE), d_c.reshape(tokens, STATE)), head_size)
    return (outputs, grad_inputs, grad_decay, grad_b, grad_c)


def solution(mesh):
    seq_size = mesh.shape["seq"]
    head_size = mesh.shape["head"]
    split = 2 if seq_size % 4 == 0 else 1
    count = seq_size // split
    grid = Mesh(mesh.devices.reshape(split, count, head_size), ("hi", "lo", "head"))
    seq = ("hi", "lo")
    placed = (P(seq, "head"), P(seq, "head"), P(seq, None), P(seq, None), P(seq, "head"))

    def body(inputs, log_decay, b_proj, c_proj, grad_out):
        return shards(inputs, log_decay, b_proj, c_proj, grad_out, count, head_size, split)

    return jax.shard_map(
        body,
        mesh=grid,
        in_specs=placed,
        out_specs=(P(seq, "head"), P(seq, "head"), P(seq, "head"), P(seq, None), P(seq, None)),
        check_vma=False,
    )
```

```python
import jax
import jax.numpy as jnp
from jax import lax
from jax.sharding import Mesh, PartitionSpec as P

HEADDIM = 64
STATE = 128
BLOCK = 256

F32 = jnp.float32
BF16 = jnp.bfloat16
HIGHEST = lax.Precision.HIGHEST


def rounded(values):
    return values.astype(BF16).astype(F32)


def split_dot(spec, exact, wide, swap=False):
    high = wide.astype(BF16)
    low = (wide - high.astype(F32)).astype(BF16)
    exact = exact.astype(BF16)
    if swap:
        return jnp.einsum(spec, high, exact, preferred_element_type=F32) + jnp.einsum(
            spec, low, exact, preferred_element_type=F32
        )
    return jnp.einsum(spec, exact, high, preferred_element_type=F32) + jnp.einsum(
        spec, exact, low, preferred_element_type=F32
    )


def gather_rows(final, state_grad, total, count):
    heads, width, state = final.shape
    share = heads * width // count
    spare = -(-heads // (8 * state)) * 8
    logs = jnp.pad(total, (0, spare * state - heads)).reshape(spare, state)
    payload = jnp.concatenate(
        [
            final.reshape(count, share, state),
            state_grad.reshape(count, share, state),
            jnp.broadcast_to(logs[None], (count, spare, state)),
        ],
        axis=1,
    )
    return lax.all_to_all(payload, "lo", 0, 0, tiled=True)


def spans_of(mask, logs):
    return jnp.exp(jnp.einsum("...k,kr->...r", mask.astype(F32), logs, precision=HIGHEST))


def scan_rows(got, heads, width, count, split):
    share = heads * width // count
    ends = got[:, :share]
    grads = got[:, share : 2 * share]
    totals = got[:, 2 * share :].reshape(count, -1)[:, :heads]
    place = lax.axis_index("lo")
    if share % width == 0:
        owned = share // width
        logs = lax.dynamic_slice_in_dim(totals, place * owned, owned, axis=1)

        def expand(a):
            return jnp.repeat(a, width, axis=-1)
    else:
        row_heads = (place * share + jnp.arange(share)) // width
        logs = jnp.take(totals, row_heads, axis=1)

        def expand(a):
            return a
    order = jnp.arange(count)
    lower = order[None, :] < order[:, None]
    between = lower.T[None, :, :] & lower[:, None, :]
    coef = expand(jnp.where(lower[:, :, None], spans_of(between, logs), 0.0))
    ahead = jnp.sum(coef[:, :, :, None] * ends[None], axis=1)
    behind = jnp.sum(coef[:, :, :, None] * grads[:, None], axis=0)
    if split > 1:
        from_start = expand(spans_of(lower, logs))[:, :, None]
        to_end = expand(spans_of(lower.T, logs))[:, :, None]
        end_state = jnp.sum(to_end * ends, axis=0)
        start_grad = jnp.sum(from_start * grads, axis=0)
        side = lax.axis_index("hi")
        sent = jnp.where(side == 0, end_state, start_grad)
        got_side = lax.ppermute(sent, "hi", [(0, 1), (1, 0)])[None]
        ahead = ahead + jnp.where(side == 1, from_start * got_side, 0.0)
        behind = behind + jnp.where(side == 0, to_end * got_side, 0.0)
    return jnp.concatenate([ahead, behind], axis=1)


def send_back(rows, heads, width, count):
    share = heads * width // count
    incoming = lax.all_to_all(rows[:, :share], "lo", 0, 0, tiled=True)
    adjoint = lax.all_to_all(rows[:, share:], "lo", 0, 0, tiled=True)
    return incoming.reshape(heads, width, STATE), adjoint.reshape(heads, width, STATE)


def head_sum(parts, size):
    if size & (size - 1):
        return lax.psum(parts, "head")
    step = 1
    while step < size:
        pairs = [(i, i ^ step) for i in range(size)]
        parts = jax.tree.map(lambda a: a + lax.ppermute(a, "head", pairs), parts)
        step *= 2
    return parts


def shards(inputs, log_decay, b_proj, c_proj, grad_out, count, head_size, split):
    tokens, head_count = log_decay.shape
    blocks = tokens // BLOCK
    x16 = inputs.reshape(blocks, BLOCK, head_count, HEADDIM).transpose(2, 0, 1, 3)
    g16 = grad_out.reshape(blocks, BLOCK, head_count, HEADDIM).transpose(2, 0, 1, 3)
    xf = x16.astype(F32)
    gf = g16.astype(F32)
    decay = log_decay.reshape(blocks, BLOCK, head_count).transpose(2, 0, 1)
    b16 = b_proj.reshape(blocks, BLOCK, STATE)
    c16 = c_proj.reshape(blocks, BLOCK, STATE)
    bf = b16.astype(F32)
    cf = c16.astype(F32)

    prefix = jnp.cumsum(decay, axis=-1)
    totals = prefix[..., -1]
    causal = jnp.tril(jnp.ones((BLOCK, BLOCK), dtype=bool))
    scores = jnp.einsum("ktn,ksn->kts", c16, b16, preferred_element_type=F32)
    spread = prefix[..., :, None] - prefix[..., None, :]
    decay_mat = jnp.where(causal, jnp.exp(jnp.where(causal, spread, 0.0)), 0.0)
    last_w = jnp.exp(totals[..., None] - prefix)
    scaled = (xf * last_w[..., None]).astype(BF16)
    states = jnp.einsum("hksp,ksn->hkpn", scaled, b16, preferred_element_type=F32)

    gain = jnp.exp(totals)
    local = jnp.zeros(states.shape[:1] + states.shape[2:], F32)
    before = []
    run_log = jnp.zeros((head_count,), F32)
    for k in range(blocks):
        before.append(run_log)
        local = gain[:, k, None, None] * local + states[:, k]
        run_log = run_log + totals[:, k]
    device_total = run_log

    e_prefix = jnp.exp(prefix)
    g_scaled = gf * e_prefix[..., None]
    start_grad = split_dot("hktp,ktn->hkpn", c16, g_scaled, swap=True)
    state_grad = start_grad[:, 0]
    for k in range(1, blocks):
        state_grad = state_grad + jnp.exp(before[k])[:, None, None] * start_grad[:, k]

    if count > 1:
        got = gather_rows(local, state_grad, device_total, count)

    weighted_f = scores[None] * decay_mat
    weighted = weighted_f.astype(BF16)
    within = jnp.einsum("hkts,hksp->hktp", weighted, x16, preferred_element_type=F32)
    d_weighted = jnp.einsum("hktp,hksp->hkts", g16, x16, preferred_element_type=F32)
    d_weighted = rounded(d_weighted)
    d_x_within = rounded(jnp.einsum("hkts,hktp->hksp", weighted, g16, preferred_element_type=F32))
    spread_grad = d_weighted * weighted_f
    d_prefix_within = jnp.sum(spread_grad, axis=-1) - jnp.sum(spread_grad, axis=-2)
    d_scores = jnp.sum(d_weighted * decay_mat, axis=0).astype(BF16)
    d_c_scores = jnp.einsum("kts,ksn->ktn", d_scores, b16, preferred_element_type=F32)
    d_b_scores = jnp.einsum("kts,ktn->ksn", d_scores, c16, preferred_element_type=F32)

    if count > 1:
        got, within, d_x_within, d_prefix_within, d_c_scores, d_b_scores = lax.optimization_barrier(
            (got, within, d_x_within, d_prefix_within, d_c_scores, d_b_scores)
        )
        rows = scan_rows(got, head_count, HEADDIM, count, split)
        incoming, adjoint = send_back(rows, head_count, HEADDIM, count)
    else:
        incoming = jnp.zeros_like(local)
        adjoint = jnp.zeros_like(local)

    starts = [incoming]
    for k in range(blocks - 1):
        starts.append(gain[:, k, None, None] * starts[-1] + states[:, k])
    start = jnp.stack(starts, axis=1)
    carried = split_dot("ktn,hkpn->hktp", c16, start)
    out = within + e_prefix[..., None] * carried
    outputs = out.transpose(1, 2, 0, 3).reshape(tokens, head_count * HEADDIM).astype(BF16)

    d_prefix = jnp.sum(g_scaled * carried, axis=-1) + d_prefix_within
    d_c = jnp.einsum("hktp,hkpn->ktn", g_scaled, start, precision=lax.Precision.HIGH) + d_c_scores

    lam = adjoint
    d_states = [None] * blocks
    d_totals = [None] * blocks
    for k in reversed(range(blocks)):
        d_states[k] = lam
        d_totals[k] = gain[:, k] * jnp.sum(lam * start[:, k], axis=(1, 2))
        lam = start_grad[:, k] + gain[:, k, None, None] * lam
    d_states = jnp.stack(d_states, axis=1)
    d_totals = jnp.stack(d_totals, axis=1)

    d_scaled = rounded(split_dot("ksn,hkpn->hksp", b16, d_states))
    d_b = split_dot("hksp,hkpn->ksn", scaled, d_states) + d_b_scores
    d_x = d_scaled * last_w[..., None] + d_x_within
    d_last = jnp.sum(d_scaled * xf, axis=-1) * last_w
    d_prefix = d_prefix - d_last
    d_totals = d_totals + jnp.sum(d_last, axis=-1)

    d_prefix = d_prefix.at[..., -1].add(d_totals)
    d_decay = lax.cumsum(d_prefix, axis=2, reverse=True)
    grad_decay = d_decay.transpose(1, 2, 0).reshape(tokens, head_count)
    grad_inputs = d_x.transpose(1, 2, 0, 3).reshape(tokens, head_count * HEADDIM).astype(BF16)
    grad_b, grad_c = head_sum((d_b.reshape(tokens, STATE), d_c.reshape(tokens, STATE)), head_size)
    return (outputs, grad_inputs, grad_decay, grad_b, grad_c)


def solution(mesh):
    seq_size = mesh.shape["seq"]
    head_size = mesh.shape["head"]
    split = 2 if seq_size % 4 == 0 else 1
    count = seq_size // split
    grid = Mesh(mesh.devices.reshape(split, count, head_size), ("hi", "lo", "head"))
    seq = ("hi", "lo")
    placed = (P(seq, "head"), P(seq, "head"), P(seq, None), P(seq, None), P(seq, "head"))

    def body(inputs, log_decay, b_proj, c_proj, grad_out):
        return shards(inputs, log_decay, b_proj, c_proj, grad_out, count, head_size, split)

    return jax.shard_map(
        body,
        mesh=grid,
        in_specs=placed,
        out_specs=(P(seq, "head"), P(seq, "head"), P(seq, "head"), P(seq, None), P(seq, None)),
        check_vma=False,
    )
```

```python
import jax
import jax.numpy as jnp
from jax import lax
from jax.sharding import Mesh, PartitionSpec as P

HEADDIM = 64
STATE = 128
BLOCK = 256

F32 = jnp.float32
BF16 = jnp.bfloat16
HIGHEST = lax.Precision.HIGHEST


def rounded(values):
    return values.astype(BF16).astype(F32)


def split_dot(spec, exact, wide, swap=False):
    high = wide.astype(BF16)
    low = (wide - high.astype(F32)).astype(BF16)
    exact = exact.astype(BF16)
    if swap:
        return jnp.einsum(spec, high, exact, preferred_element_type=F32) + jnp.einsum(
            spec, low, exact, preferred_element_type=F32
        )
    return jnp.einsum(spec, exact, high, preferred_element_type=F32) + jnp.einsum(
        spec, exact, low, preferred_element_type=F32
    )


def gather_rows(final, state_grad, total, count):
    heads, width, state = final.shape
    share = heads * width // count
    spare = -(-heads // (8 * state)) * 8
    logs = jnp.pad(total, (0, spare * state - heads)).reshape(spare, state)
    payload = jnp.concatenate(
        [
            final.reshape(count, share, state),
            state_grad.reshape(count, share, state),
            jnp.broadcast_to(logs[None], (count, spare, state)),
        ],
        axis=1,
    )
    return lax.all_to_all(payload, "lo", 0, 0, tiled=True)


def spans_of(mask, logs):
    return jnp.exp(jnp.einsum("...k,kr->...r", mask.astype(F32), logs, precision=HIGHEST))


def scan_rows(got, heads, width, count, split):
    share = heads * width // count
    ends = got[:, :share]
    grads = got[:, share : 2 * share]
    totals = got[:, 2 * share :].reshape(count, -1)[:, :heads]
    place = lax.axis_index("lo")
    if share % width == 0:
        owned = share // width
        logs = lax.dynamic_slice_in_dim(totals, place * owned, owned, axis=1)
        logs = jnp.repeat(logs, width, axis=1)
    else:
        row_heads = (place * share + jnp.arange(share)) // width
        logs = jnp.take(totals, row_heads, axis=1)
    order = jnp.arange(count)
    lower = order[None, :] < order[:, None]
    between = lower.T[None, :, :] & lower[:, None, :]
    coef = jnp.where(lower[:, :, None], spans_of(between, logs), 0.0)
    ahead = jnp.sum(coef[:, :, :, None] * ends[None], axis=1)
    behind = jnp.sum(coef[:, :, :, None] * grads[:, None], axis=0)
    if split > 1:
        from_start = spans_of(lower, logs)[:, :, None]
        to_end = spans_of(lower.T, logs)[:, :, None]
        end_state = jnp.sum(to_end * ends, axis=0)
        start_grad = jnp.sum(from_start * grads, axis=0)
        side = lax.axis_index("hi")
        sent = jnp.where(side == 0, end_state, start_grad)
        got_side = lax.ppermute(sent, "hi", [(0, 1), (1, 0)])[None]
        ahead = ahead + jnp.where(side == 1, from_start * got_side, 0.0)
        behind = behind + jnp.where(side == 0, to_end * got_side, 0.0)
    return jnp.concatenate([ahead, behind], axis=1)


def send_back(rows, heads, width, count):
    share = heads * width // count
    incoming = lax.all_to_all(rows[:, :share], "lo", 0, 0, tiled=True)
    adjoint = lax.all_to_all(rows[:, share:], "lo", 0, 0, tiled=True)
    return incoming.reshape(heads, width, STATE), adjoint.reshape(heads, width, STATE)


def head_sum(parts, size):
    if size & (size - 1):
        return lax.psum(parts, "head")
    step = 1
    while step < size:
        pairs = [(i, i ^ step) for i in range(size)]
        parts = jax.tree.map(lambda a: a + lax.ppermute(a, "head", pairs), parts)
        step *= 2
    return parts


def shards(inputs, log_decay, b_proj, c_proj, grad_out, count, head_size, split):
    tokens, head_count = log_decay.shape
    blocks = tokens // BLOCK
    x16 = inputs.reshape(blocks, BLOCK, head_count, HEADDIM).transpose(2, 0, 1, 3)
    g16 = grad_out.reshape(blocks, BLOCK, head_count, HEADDIM).transpose(2, 0, 1, 3)
    xf = x16.astype(F32)
    gf = g16.astype(F32)
    decay = log_decay.reshape(blocks, BLOCK, head_count).transpose(2, 0, 1)
    b16 = b_proj.reshape(blocks, BLOCK, STATE)
    c16 = c_proj.reshape(blocks, BLOCK, STATE)
    bf = b16.astype(F32)
    cf = c16.astype(F32)

    prefix = jnp.cumsum(decay, axis=-1)
    totals = prefix[..., -1]
    causal = jnp.tril(jnp.ones((BLOCK, BLOCK), dtype=bool))
    scores = jnp.einsum("ktn,ksn->kts", c16, b16, preferred_element_type=F32)
    spread = prefix[..., :, None] - prefix[..., None, :]
    decay_mat = jnp.where(causal, jnp.exp(jnp.where(causal, spread, 0.0)), 0.0)
    last_w = jnp.exp(totals[..., None] - prefix)
    scaled = (xf * last_w[..., None]).astype(BF16)
    states = jnp.einsum("hksp,ksn->hkpn", scaled, b16, preferred_element_type=F32)

    gain = jnp.exp(totals)
    local = jnp.zeros(states.shape[:1] + states.shape[2:], F32)
    before = []
    run_log = jnp.zeros((head_count,), F32)
    for k in range(blocks):
        before.append(run_log)
        local = gain[:, k, None, None] * local + states[:, k]
        run_log = run_log + totals[:, k]
    device_total = run_log

    e_prefix = jnp.exp(prefix)
    g_scaled = gf * e_prefix[..., None]
    start_grad = split_dot("hktp,ktn->hkpn", c16, g_scaled, swap=True)
    state_grad = start_grad[:, 0]
    for k in range(1, blocks):
        state_grad = state_grad + jnp.exp(before[k])[:, None, None] * start_grad[:, k]

    if count > 1:
        got = gather_rows(local, state_grad, device_total, count)

    weighted_f = scores[None] * decay_mat
    weighted = weighted_f.astype(BF16)
    within = jnp.einsum("hkts,hksp->hktp", weighted, x16, preferred_element_type=F32)
    d_weighted = jnp.einsum("hktp,hksp->hkts", g16, x16, preferred_element_type=F32)
    d_weighted = rounded(d_weighted)
    d_x_within = rounded(jnp.einsum("hkts,hktp->hksp", weighted, g16, preferred_element_type=F32))
    spread_grad = d_weighted * weighted_f
    d_prefix_within = jnp.sum(spread_grad, axis=-1) - jnp.sum(spread_grad, axis=-2)
    d_scores = jnp.sum(d_weighted * decay_mat, axis=0).astype(BF16)
    d_c_scores = jnp.einsum("kts,ksn->ktn", d_scores, b16, preferred_element_type=F32)
    d_b_scores = jnp.einsum("kts,ktn->ksn", d_scores, c16, preferred_element_type=F32)

    if count > 1:
        got, within, d_x_within, d_prefix_within, d_c_scores, d_b_scores = lax.optimization_barrier(
            (got, within, d_x_within, d_prefix_within, d_c_scores, d_b_scores)
        )
        rows = scan_rows(got, head_count, HEADDIM, count, split)
        incoming, adjoint = send_back(rows, head_count, HEADDIM, count)
    else:
        incoming = jnp.zeros_like(local)
        adjoint = jnp.zeros_like(local)

    starts = [incoming]
    for k in range(blocks - 1):
        starts.append(gain[:, k, None, None] * starts[-1] + states[:, k])
    start = jnp.stack(starts, axis=1)
    carried = split_dot("ktn,hkpn->hktp", c16, start)
    out = within + e_prefix[..., None] * carried
    outputs = out.transpose(1, 2, 0, 3).reshape(tokens, head_count * HEADDIM).astype(BF16)

    d_prefix = jnp.sum(g_scaled * carried, axis=-1) + d_prefix_within
    g_high = g_scaled.astype(BF16)
    g_low = (g_scaled - g_high.astype(F32)).astype(BF16)
    s_high = start.astype(BF16)
    s_low = (start - s_high.astype(F32)).astype(BF16)
    d_c = d_c_scores
    for left, right in ((g_high, s_high), (g_high, s_low), (g_low, s_high)):
        d_c = d_c + jnp.einsum("hktp,hkpn->ktn", left, right, preferred_element_type=F32)

    lam = adjoint
    d_states = [None] * blocks
    d_totals = [None] * blocks
    for k in reversed(range(blocks)):
        d_states[k] = lam
        d_totals[k] = gain[:, k] * jnp.sum(lam * start[:, k], axis=(1, 2))
        lam = start_grad[:, k] + gain[:, k, None, None] * lam
    d_states = jnp.stack(d_states, axis=1)
    d_totals = jnp.stack(d_totals, axis=1)

    d_scaled = rounded(split_dot("ksn,hkpn->hksp", b16, d_states))
    d_b = split_dot("hksp,hkpn->ksn", scaled, d_states) + d_b_scores
    d_x = d_scaled * last_w[..., None] + d_x_within
    d_last = jnp.sum(d_scaled * xf, axis=-1) * last_w
    d_prefix = d_prefix - d_last
    d_totals = d_totals + jnp.sum(d_last, axis=-1)

    d_prefix = d_prefix.at[..., -1].add(d_totals)
    d_decay = lax.cumsum(d_prefix, axis=2, reverse=True)
    grad_decay = d_decay.transpose(1, 2, 0).reshape(tokens, head_count)
    grad_inputs = d_x.transpose(1, 2, 0, 3).reshape(tokens, head_count * HEADDIM).astype(BF16)
    grad_b, grad_c = head_sum((d_b.reshape(tokens, STATE), d_c.reshape(tokens, STATE)), head_size)
    return (outputs, grad_inputs, grad_decay, grad_b, grad_c)


def solution(mesh):
    seq_size = mesh.shape["seq"]
    head_size = mesh.shape["head"]
    split = 2 if seq_size % 4 == 0 else 1
    count = seq_size // split
    grid = Mesh(mesh.devices.reshape(split, count, head_size), ("hi", "lo", "head"))
    seq = ("hi", "lo")
    placed = (P(seq, "head"), P(seq, "head"), P(seq, None), P(seq, None), P(seq, "head"))

    def body(inputs, log_decay, b_proj, c_proj, grad_out):
        return shards(inputs, log_decay, b_proj, c_proj, grad_out, count, head_size, split)

    return jax.shard_map(
        body,
        mesh=grid,
        in_specs=placed,
        out_specs=(P(seq, "head"), P(seq, "head"), P(seq, "head"), P(seq, None), P(seq, None)),
        check_vma=False,
    )
```

```python
import jax
import jax.numpy as jnp
from jax import lax
from jax.sharding import Mesh, PartitionSpec as P

HEADDIM = 64
STATE = 128
BLOCK = 256

F32 = jnp.float32
BF16 = jnp.bfloat16
HIGHEST = lax.Precision.HIGHEST


def rounded(values):
    return values.astype(BF16).astype(F32)


def split_dot(spec, exact, wide, swap=False):
    high = wide.astype(BF16)
    low = (wide - high.astype(F32)).astype(BF16)
    exact = exact.astype(BF16)
    if swap:
        return jnp.einsum(spec, high, exact, preferred_element_type=F32) + jnp.einsum(
            spec, low, exact, preferred_element_type=F32
        )
    return jnp.einsum(spec, exact, high, preferred_element_type=F32) + jnp.einsum(
        spec, exact, low, preferred_element_type=F32
    )


def gather_rows(final, state_grad, total, count):
    heads, width, state = final.shape
    share = heads * width // count
    spare = -(-heads // (8 * state)) * 8
    logs = jnp.pad(total, (0, spare * state - heads)).reshape(spare, state)
    payload = jnp.concatenate(
        [
            final.reshape(count, share, state),
            state_grad.reshape(count, share, state),
            jnp.broadcast_to(logs[None], (count, spare, state)),
        ],
        axis=1,
    )
    return lax.all_to_all(payload, "lo", 0, 0, tiled=True)


def spans_of(mask, logs):
    return jnp.exp(jnp.einsum("...k,kr->...r", mask.astype(F32), logs, precision=HIGHEST))


def scan_rows(got, heads, width, count, split):
    share = heads * width // count
    ends = got[:, :share]
    grads = got[:, share : 2 * share]
    totals = got[:, 2 * share :].reshape(count, -1)[:, :heads]
    place = lax.axis_index("lo")
    if share % width == 0:
        owned = share // width
        logs = lax.dynamic_slice_in_dim(totals, place * owned, owned, axis=1)
        logs = jnp.repeat(logs, width, axis=1)
    else:
        row_heads = (place * share + jnp.arange(share)) // width
        logs = jnp.take(totals, row_heads, axis=1)
    order = jnp.arange(count)
    lower = order[None, :] < order[:, None]
    between = lower.T[None, :, :] & lower[:, None, :]
    coef = jnp.where(lower[:, :, None], spans_of(between, logs), 0.0)
    ahead = jnp.sum(coef[:, :, :, None] * ends[None], axis=1)
    behind = jnp.sum(coef[:, :, :, None] * grads[:, None], axis=0)
    if split > 1:
        from_start = spans_of(lower, logs)[:, :, None]
        to_end = spans_of(lower.T, logs)[:, :, None]
        end_state = jnp.sum(to_end * ends, axis=0)
        start_grad = jnp.sum(from_start * grads, axis=0)
        side = lax.axis_index("hi")
        sent = jnp.where(side == 0, end_state, start_grad)
        got_side = lax.ppermute(sent, "hi", [(0, 1), (1, 0)])[None]
        ahead = ahead + jnp.where(side == 1, from_start * got_side, 0.0)
        behind = behind + jnp.where(side == 0, to_end * got_side, 0.0)
    return jnp.concatenate([ahead, behind], axis=1)


def send_back(rows, heads, width, count):
    share = heads * width // count
    incoming = lax.all_to_all(rows[:, :share], "lo", 0, 0, tiled=True)
    adjoint = lax.all_to_all(rows[:, share:], "lo", 0, 0, tiled=True)
    return incoming.reshape(heads, width, STATE), adjoint.reshape(heads, width, STATE)


def head_sum(parts, size):
    if size & (size - 1):
        return lax.psum(parts, "head")
    step = 1
    while step < size:
        pairs = [(i, i ^ step) for i in range(size)]
        parts = jax.tree.map(lambda a: a + lax.ppermute(a, "head", pairs), parts)
        step *= 2
    return parts


def shards(inputs, log_decay, b_proj, c_proj, grad_out, count, head_size, split):
    tokens, head_count = log_decay.shape
    blocks = tokens // BLOCK
    x16 = inputs.reshape(blocks, BLOCK, head_count, HEADDIM).transpose(2, 0, 1, 3)
    g16 = grad_out.reshape(blocks, BLOCK, head_count, HEADDIM).transpose(2, 0, 1, 3)
    xf = x16.astype(F32)
    gf = g16.astype(F32)
    decay = log_decay.reshape(blocks, BLOCK, head_count).transpose(2, 0, 1)
    b16 = b_proj.reshape(blocks, BLOCK, STATE)
    c16 = c_proj.reshape(blocks, BLOCK, STATE)
    bf = b16.astype(F32)
    cf = c16.astype(F32)

    prefix = jnp.cumsum(decay, axis=-1)
    totals = prefix[..., -1]
    causal = jnp.tril(jnp.ones((BLOCK, BLOCK), dtype=bool))
    scores = jnp.einsum("ktn,ksn->kts", c16, b16, preferred_element_type=F32)
    spread = prefix[..., :, None] - prefix[..., None, :]
    decay_mat = jnp.where(causal, jnp.exp(jnp.where(causal, spread, 0.0)), 0.0)
    last_w = jnp.exp(totals[..., None] - prefix)
    scaled = (xf * last_w[..., None]).astype(BF16)
    states = jnp.einsum("hksp,ksn->hkpn", scaled, b16, preferred_element_type=F32)

    gain = jnp.exp(totals)
    local = jnp.zeros(states.shape[:1] + states.shape[2:], F32)
    before = []
    run_log = jnp.zeros((head_count,), F32)
    for k in range(blocks):
        before.append(run_log)
        local = gain[:, k, None, None] * local + states[:, k]
        run_log = run_log + totals[:, k]
    device_total = run_log

    e_prefix = jnp.exp(prefix)
    g_scaled = gf * e_prefix[..., None]
    start_grad = split_dot("hktp,ktn->hkpn", c16, g_scaled, swap=True)
    state_grad = start_grad[:, 0]
    for k in range(1, blocks):
        state_grad = state_grad + jnp.exp(before[k])[:, None, None] * start_grad[:, k]

    if count > 1:
        got = gather_rows(local, state_grad, device_total, count)

    weighted_f = scores[None] * decay_mat
    weighted = weighted_f.astype(BF16)
    within = jnp.einsum("hkts,hksp->hktp", weighted, x16, preferred_element_type=F32)
    d_weighted = jnp.einsum("hktp,hksp->hkts", g16, x16, preferred_element_type=F32)
    d_weighted = rounded(d_weighted)
    d_x_within = rounded(jnp.einsum("hkts,hktp->hksp", weighted, g16, preferred_element_type=F32))
    spread_grad = d_weighted * weighted_f
    d_prefix_within = jnp.sum(spread_grad, axis=-1) - jnp.sum(spread_grad, axis=-2)
    d_scores = jnp.sum(d_weighted * decay_mat, axis=0).astype(BF16)
    d_c_scores = jnp.einsum("kts,ksn->ktn", d_scores, b16, preferred_element_type=F32)
    d_b_scores = jnp.einsum("kts,ktn->ksn", d_scores, c16, preferred_element_type=F32)

    if count > 1:
        got, within, d_x_within, d_prefix_within, d_c_scores, d_b_scores = lax.optimization_barrier(
            (got, within, d_x_within, d_prefix_within, d_c_scores, d_b_scores)
        )
        rows = scan_rows(got, head_count, HEADDIM, count, split)
        incoming, adjoint = send_back(rows, head_count, HEADDIM, count)
    else:
        incoming = jnp.zeros_like(local)
        adjoint = jnp.zeros_like(local)

    starts = [incoming]
    for k in range(blocks - 1):
        starts.append(gain[:, k, None, None] * starts[-1] + states[:, k])
    start = jnp.stack(starts, axis=1)
    carried = split_dot("ktn,hkpn->hktp", c16, start)
    out = within + e_prefix[..., None] * carried
    outputs = out.transpose(1, 2, 0, 3).reshape(tokens, head_count * HEADDIM).astype(BF16)

    d_prefix = jnp.sum(g_scaled * carried, axis=-1) + d_prefix_within
    d_c = jnp.einsum("hktp,hkpn->ktn", g_scaled, start, precision=lax.Precision.HIGH) + d_c_scores

    lam = adjoint
    d_states = [None] * blocks
    d_totals = [None] * blocks
    for k in reversed(range(blocks)):
        d_states[k] = lam
        d_totals[k] = gain[:, k] * jnp.sum(lam * start[:, k], axis=(1, 2))
        lam = start_grad[:, k] + gain[:, k, None, None] * lam
    d_states = jnp.stack(d_states, axis=1)
    d_totals = jnp.stack(d_totals, axis=1)

    d_scaled = rounded(split_dot("ksn,hkpn->hksp", b16, d_states))
    d_b = split_dot("hksp,hkpn->ksn", scaled, d_states) + d_b_scores
    d_x = d_scaled * last_w[..., None] + d_x_within
    d_last = jnp.sum(d_scaled * xf, axis=-1) * last_w
    d_prefix = d_prefix - d_last
    d_totals = d_totals + jnp.sum(d_last, axis=-1)

    d_prefix = d_prefix.at[..., -1].add(d_totals)
    d_decay = lax.cumsum(d_prefix, axis=2, reverse=True)
    grad_decay = d_decay.transpose(1, 2, 0).reshape(tokens, head_count)
    grad_inputs = d_x.transpose(1, 2, 0, 3).reshape(tokens, head_count * HEADDIM).astype(BF16)
    both = head_sum(jnp.concatenate([d_b.reshape(tokens, STATE), d_c.reshape(tokens, STATE)], axis=1), head_size)
    grad_b, grad_c = both[:, :STATE], both[:, STATE:]
    return (outputs, grad_inputs, grad_decay, grad_b, grad_c)


def solution(mesh):
    seq_size = mesh.shape["seq"]
    head_size = mesh.shape["head"]
    split = 2 if seq_size % 4 == 0 else 1
    count = seq_size // split
    grid = Mesh(mesh.devices.reshape(split, count, head_size), ("hi", "lo", "head"))
    seq = ("hi", "lo")
    placed = (P(seq, "head"), P(seq, "head"), P(seq, None), P(seq, None), P(seq, "head"))

    def body(inputs, log_decay, b_proj, c_proj, grad_out):
        return shards(inputs, log_decay, b_proj, c_proj, grad_out, count, head_size, split)

    return jax.shard_map(
        body,
        mesh=grid,
        in_specs=placed,
        out_specs=(P(seq, "head"), P(seq, "head"), P(seq, "head"), P(seq, None), P(seq, None)),
        check_vma=False,
    )
```

```python
import jax
import jax.numpy as jnp
from jax import lax
from jax.sharding import Mesh, PartitionSpec as P

HEADDIM = 64
STATE = 128
BLOCK = 256

F32 = jnp.float32
BF16 = jnp.bfloat16
HIGHEST = lax.Precision.HIGHEST


def rounded(values):
    return values.astype(BF16).astype(F32)


def split_dot(spec, exact, wide, swap=False):
    high = wide.astype(BF16)
    low = (wide - high.astype(F32)).astype(BF16)
    exact = exact.astype(BF16)
    if swap:
        return jnp.einsum(spec, high, exact, preferred_element_type=F32) + jnp.einsum(
            spec, low, exact, preferred_element_type=F32
        )
    return jnp.einsum(spec, exact, high, preferred_element_type=F32) + jnp.einsum(
        spec, exact, low, preferred_element_type=F32
    )


def gather_rows(final, state_grad, total, count):
    heads, width, state = final.shape
    share = heads * width // count
    spare = -(-heads // (8 * state)) * 8
    logs = jnp.pad(total, (0, spare * state - heads)).reshape(spare, state)
    payload = jnp.concatenate(
        [
            final.reshape(count, share, state),
            state_grad.reshape(count, share, state),
            jnp.broadcast_to(logs[None], (count, spare, state)),
        ],
        axis=1,
    )
    return lax.all_to_all(payload, "lo", 0, 0, tiled=True)


def spans_of(mask, logs):
    return jnp.exp(jnp.einsum("...k,kr->...r", mask.astype(F32), logs, precision=HIGHEST))


def scan_rows(got, heads, width, count, split):
    share = heads * width // count
    ends = got[:, :share]
    grads = got[:, share : 2 * share]
    totals = got[:, 2 * share :].reshape(count, -1)[:, :heads]
    place = lax.axis_index("lo")
    if share % width == 0:
        owned = share // width
        logs = lax.dynamic_slice_in_dim(totals, place * owned, owned, axis=1)
        logs = jnp.repeat(logs, width, axis=1)
    else:
        row_heads = (place * share + jnp.arange(share)) // width
        logs = jnp.take(totals, row_heads, axis=1)
    order = jnp.arange(count)
    lower = order[None, :] < order[:, None]
    between = lower.T[None, :, :] & lower[:, None, :]
    coef = jnp.where(lower[:, :, None], spans_of(between, logs), 0.0)
    ahead = jnp.sum(coef[:, :, :, None] * ends[None], axis=1)
    behind = jnp.sum(coef[:, :, :, None] * grads[:, None], axis=0)
    if split > 1:
        from_start = spans_of(lower, logs)[:, :, None]
        to_end = spans_of(lower.T, logs)[:, :, None]
        side = lax.axis_index("hi")
        left = side == 0
        sent = jnp.sum(jnp.where(left, to_end, from_start) * jnp.where(left, ends, grads), axis=0)
        got_side = lax.ppermute(sent, "hi", [(0, 1), (1, 0)])[None]
        ahead = ahead + jnp.where(side == 1, from_start * got_side, 0.0)
        behind = behind + jnp.where(side == 0, to_end * got_side, 0.0)
    return jnp.concatenate([ahead, behind], axis=1)


def send_back(rows, heads, width, count):
    share = heads * width // count
    incoming = lax.all_to_all(rows[:, :share], "lo", 0, 0, tiled=True)
    adjoint = lax.all_to_all(rows[:, share:], "lo", 0, 0, tiled=True)
    return incoming.reshape(heads, width, STATE), adjoint.reshape(heads, width, STATE)


def head_sum(parts, size):
    if size & (size - 1):
        return lax.psum(parts, "head")
    step = 1
    while step < size:
        pairs = [(i, i ^ step) for i in range(size)]
        parts = jax.tree.map(lambda a: a + lax.ppermute(a, "head", pairs), parts)
        step *= 2
    return parts


def shards(inputs, log_decay, b_proj, c_proj, grad_out, count, head_size, split):
    tokens, head_count = log_decay.shape
    blocks = tokens // BLOCK
    x16 = inputs.reshape(blocks, BLOCK, head_count, HEADDIM).transpose(2, 0, 1, 3)
    g16 = grad_out.reshape(blocks, BLOCK, head_count, HEADDIM).transpose(2, 0, 1, 3)
    xf = x16.astype(F32)
    gf = g16.astype(F32)
    decay = log_decay.reshape(blocks, BLOCK, head_count).transpose(2, 0, 1)
    b16 = b_proj.reshape(blocks, BLOCK, STATE)
    c16 = c_proj.reshape(blocks, BLOCK, STATE)
    bf = b16.astype(F32)
    cf = c16.astype(F32)

    prefix = jnp.cumsum(decay, axis=-1)
    totals = prefix[..., -1]
    causal = jnp.tril(jnp.ones((BLOCK, BLOCK), dtype=bool))
    scores = jnp.einsum("ktn,ksn->kts", c16, b16, preferred_element_type=F32)
    spread = prefix[..., :, None] - prefix[..., None, :]
    decay_mat = jnp.where(causal, jnp.exp(jnp.where(causal, spread, 0.0)), 0.0)
    last_w = jnp.exp(totals[..., None] - prefix)
    scaled = (xf * last_w[..., None]).astype(BF16)
    states = jnp.einsum("hksp,ksn->hkpn", scaled, b16, preferred_element_type=F32)

    gain = jnp.exp(totals)
    local = jnp.zeros(states.shape[:1] + states.shape[2:], F32)
    before = []
    run_log = jnp.zeros((head_count,), F32)
    for k in range(blocks):
        before.append(run_log)
        local = gain[:, k, None, None] * local + states[:, k]
        run_log = run_log + totals[:, k]
    device_total = run_log

    e_prefix = jnp.exp(prefix)
    g_scaled = gf * e_prefix[..., None]
    start_grad = split_dot("hktp,ktn->hkpn", c16, g_scaled, swap=True)
    state_grad = start_grad[:, 0]
    for k in range(1, blocks):
        state_grad = state_grad + jnp.exp(before[k])[:, None, None] * start_grad[:, k]

    if count > 1:
        got = gather_rows(local, state_grad, device_total, count)

    weighted_f = scores[None] * decay_mat
    weighted = weighted_f.astype(BF16)
    within = jnp.einsum("hkts,hksp->hktp", weighted, x16, preferred_element_type=F32)
    d_weighted = jnp.einsum("hktp,hksp->hkts", g16, x16, preferred_element_type=F32)
    d_weighted = rounded(d_weighted)
    d_x_within = rounded(jnp.einsum("hkts,hktp->hksp", weighted, g16, preferred_element_type=F32))
    spread_grad = d_weighted * weighted_f
    d_prefix_within = jnp.sum(spread_grad, axis=-1) - jnp.sum(spread_grad, axis=-2)
    d_scores = jnp.sum(d_weighted * decay_mat, axis=0).astype(BF16)
    d_c_scores = jnp.einsum("kts,ksn->ktn", d_scores, b16, preferred_element_type=F32)
    d_b_scores = jnp.einsum("kts,ktn->ksn", d_scores, c16, preferred_element_type=F32)

    if count > 1:
        got, within, d_x_within, d_prefix_within, d_c_scores, d_b_scores = lax.optimization_barrier(
            (got, within, d_x_within, d_prefix_within, d_c_scores, d_b_scores)
        )
        rows = scan_rows(got, head_count, HEADDIM, count, split)
        incoming, adjoint = send_back(rows, head_count, HEADDIM, count)
    else:
        incoming = jnp.zeros_like(local)
        adjoint = jnp.zeros_like(local)

    starts = [incoming]
    for k in range(blocks - 1):
        starts.append(gain[:, k, None, None] * starts[-1] + states[:, k])
    start = jnp.stack(starts, axis=1)
    carried = split_dot("ktn,hkpn->hktp", c16, start)
    out = within + e_prefix[..., None] * carried
    outputs = out.transpose(1, 2, 0, 3).reshape(tokens, head_count * HEADDIM).astype(BF16)

    d_prefix = jnp.sum(g_scaled * carried, axis=-1) + d_prefix_within
    d_c = jnp.einsum("hktp,hkpn->ktn", g_scaled, start, precision=lax.Precision.HIGH) + d_c_scores

    lam = adjoint
    d_states = [None] * blocks
    d_totals = [None] * blocks
    for k in reversed(range(blocks)):
        d_states[k] = lam
        d_totals[k] = gain[:, k] * jnp.sum(lam * start[:, k], axis=(1, 2))
        lam = start_grad[:, k] + gain[:, k, None, None] * lam
    d_states = jnp.stack(d_states, axis=1)
    d_totals = jnp.stack(d_totals, axis=1)

    d_scaled = rounded(split_dot("ksn,hkpn->hksp", b16, d_states))
    d_b = split_dot("hksp,hkpn->ksn", scaled, d_states) + d_b_scores
    d_x = d_scaled * last_w[..., None] + d_x_within
    d_last = jnp.sum(d_scaled * xf, axis=-1) * last_w
    d_prefix = d_prefix - d_last
    d_totals = d_totals + jnp.sum(d_last, axis=-1)

    d_prefix = d_prefix.at[..., -1].add(d_totals)
    d_decay = lax.cumsum(d_prefix, axis=2, reverse=True)
    grad_decay = d_decay.transpose(1, 2, 0).reshape(tokens, head_count)
    grad_inputs = d_x.transpose(1, 2, 0, 3).reshape(tokens, head_count * HEADDIM).astype(BF16)
    grad_b, grad_c = head_sum((d_b.reshape(tokens, STATE), d_c.reshape(tokens, STATE)), head_size)
    return (outputs, grad_inputs, grad_decay, grad_b, grad_c)


def solution(mesh):
    seq_size = mesh.shape["seq"]
    head_size = mesh.shape["head"]
    split = 2 if seq_size % 4 == 0 else 1
    count = seq_size // split
    grid = Mesh(mesh.devices.reshape(split, count, head_size), ("hi", "lo", "head"))
    seq = ("hi", "lo")
    placed = (P(seq, "head"), P(seq, "head"), P(seq, None), P(seq, None), P(seq, "head"))

    def body(inputs, log_decay, b_proj, c_proj, grad_out):
        return shards(inputs, log_decay, b_proj, c_proj, grad_out, count, head_size, split)

    return jax.shard_map(
        body,
        mesh=grid,
        in_specs=placed,
        out_specs=(P(seq, "head"), P(seq, "head"), P(seq, "head"), P(seq, None), P(seq, None)),
        check_vma=False,
    )
```

```python
import jax
import jax.numpy as jnp
from jax import lax
from jax.sharding import Mesh, PartitionSpec as P

HEADDIM = 64
STATE = 128
BLOCK = 256

F32 = jnp.float32
BF16 = jnp.bfloat16
HIGHEST = lax.Precision.HIGHEST


def rounded(values):
    return values.astype(BF16).astype(F32)


def split_dot(spec, exact, wide, swap=False):
    high = wide.astype(BF16)
    low = (wide - high.astype(F32)).astype(BF16)
    exact = exact.astype(BF16)
    if swap:
        return jnp.einsum(spec, high, exact, preferred_element_type=F32) + jnp.einsum(
            spec, low, exact, preferred_element_type=F32
        )
    return jnp.einsum(spec, exact, high, preferred_element_type=F32) + jnp.einsum(
        spec, exact, low, preferred_element_type=F32
    )


def gather_rows(final, state_grad, total, count):
    heads, width, state = final.shape
    share = heads * width // count
    spare = -(-heads // (8 * state)) * 8
    logs = jnp.pad(total, (0, spare * state - heads)).reshape(spare, state)
    payload = jnp.concatenate(
        [
            final.reshape(count, share, state),
            state_grad.reshape(count, share, state),
            jnp.broadcast_to(logs[None], (count, spare, state)),
        ],
        axis=1,
    )
    return lax.all_to_all(payload, "lo", 0, 0, tiled=True)


def spans_of(mask, logs):
    return jnp.exp(jnp.einsum("...k,kr->...r", mask.astype(F32), logs, precision=HIGHEST))


def scan_rows(got, heads, width, count, split):
    share = heads * width // count
    ends = got[:, :share]
    grads = got[:, share : 2 * share]
    totals = got[:, 2 * share :].reshape(count, -1)[:, :heads]
    place = lax.axis_index("lo")
    if share % width == 0:
        owned = share // width
        logs = lax.dynamic_slice_in_dim(totals, place * owned, owned, axis=1)
        logs = jnp.repeat(logs, width, axis=1)
    else:
        row_heads = (place * share + jnp.arange(share)) // width
        logs = jnp.take(totals, row_heads, axis=1)
    order = jnp.arange(count)
    lower = order[None, :] < order[:, None]
    between = lower.T[None, :, :] & lower[:, None, :]
    coef = jnp.where(lower[:, :, None], spans_of(between, logs), 0.0)
    ahead = jnp.sum(coef[:, :, :, None] * ends[None], axis=1)
    behind = jnp.sum(coef[:, :, :, None] * grads[:, None], axis=0)
    if split > 1:
        through = jnp.cumsum(logs, axis=0)
        from_start = jnp.exp(through - logs)[:, :, None]
        to_end = jnp.exp(lax.cumsum(logs, axis=0, reverse=True) - logs)[:, :, None]
        end_state = jnp.sum(to_end * ends, axis=0)
        start_grad = jnp.sum(from_start * grads, axis=0)
        side = lax.axis_index("hi")
        sent = jnp.where(side == 0, end_state, start_grad)
        got_side = lax.ppermute(sent, "hi", [(0, 1), (1, 0)])[None]
        ahead = ahead + jnp.where(side == 1, from_start * got_side, 0.0)
        behind = behind + jnp.where(side == 0, to_end * got_side, 0.0)
    return jnp.concatenate([ahead, behind], axis=1)


def send_back(rows, heads, width, count):
    share = heads * width // count
    incoming = lax.all_to_all(rows[:, :share], "lo", 0, 0, tiled=True)
    adjoint = lax.all_to_all(rows[:, share:], "lo", 0, 0, tiled=True)
    return incoming.reshape(heads, width, STATE), adjoint.reshape(heads, width, STATE)


def head_sum(parts, size):
    if size & (size - 1):
        return lax.psum(parts, "head")
    step = 1
    while step < size:
        pairs = [(i, i ^ step) for i in range(size)]
        parts = jax.tree.map(lambda a: a + lax.ppermute(a, "head", pairs), parts)
        step *= 2
    return parts


def shards(inputs, log_decay, b_proj, c_proj, grad_out, count, head_size, split):
    tokens, head_count = log_decay.shape
    blocks = tokens // BLOCK
    x16 = inputs.reshape(blocks, BLOCK, head_count, HEADDIM).transpose(2, 0, 1, 3)
    g16 = grad_out.reshape(blocks, BLOCK, head_count, HEADDIM).transpose(2, 0, 1, 3)
    xf = x16.astype(F32)
    gf = g16.astype(F32)
    decay = log_decay.reshape(blocks, BLOCK, head_count).transpose(2, 0, 1)
    b16 = b_proj.reshape(blocks, BLOCK, STATE)
    c16 = c_proj.reshape(blocks, BLOCK, STATE)
    bf = b16.astype(F32)
    cf = c16.astype(F32)

    prefix = jnp.cumsum(decay, axis=-1)
    totals = prefix[..., -1]
    causal = jnp.tril(jnp.ones((BLOCK, BLOCK), dtype=bool))
    scores = jnp.einsum("ktn,ksn->kts", c16, b16, preferred_element_type=F32)
    spread = prefix[..., :, None] - prefix[..., None, :]
    decay_mat = jnp.where(causal, jnp.exp(jnp.where(causal, spread, 0.0)), 0.0)
    last_w = jnp.exp(totals[..., None] - prefix)
    scaled = (xf * last_w[..., None]).astype(BF16)
    states = jnp.einsum("hksp,ksn->hkpn", scaled, b16, preferred_element_type=F32)

    gain = jnp.exp(totals)
    local = jnp.zeros(states.shape[:1] + states.shape[2:], F32)
    before = []
    run_log = jnp.zeros((head_count,), F32)
    for k in range(blocks):
        before.append(run_log)
        local = gain[:, k, None, None] * local + states[:, k]
        run_log = run_log + totals[:, k]
    device_total = run_log

    e_prefix = jnp.exp(prefix)
    g_scaled = gf * e_prefix[..., None]
    start_grad = split_dot("hktp,ktn->hkpn", c16, g_scaled, swap=True)
    state_grad = start_grad[:, 0]
    for k in range(1, blocks):
        state_grad = state_grad + jnp.exp(before[k])[:, None, None] * start_grad[:, k]

    if count > 1:
        got = gather_rows(local, state_grad, device_total, count)

    weighted_f = scores[None] * decay_mat
    weighted = weighted_f.astype(BF16)
    within = jnp.einsum("hkts,hksp->hktp", weighted, x16, preferred_element_type=F32)
    d_weighted = jnp.einsum("hktp,hksp->hkts", g16, x16, preferred_element_type=F32)
    d_weighted = rounded(d_weighted)
    d_x_within = rounded(jnp.einsum("hkts,hktp->hksp", weighted, g16, preferred_element_type=F32))
    spread_grad = d_weighted * weighted_f
    d_prefix_within = jnp.sum(spread_grad, axis=-1) - jnp.sum(spread_grad, axis=-2)
    d_scores = jnp.sum(d_weighted * decay_mat, axis=0).astype(BF16)
    d_c_scores = jnp.einsum("kts,ksn->ktn", d_scores, b16, preferred_element_type=F32)
    d_b_scores = jnp.einsum("kts,ktn->ksn", d_scores, c16, preferred_element_type=F32)

    if count > 1:
        got, within, d_x_within, d_prefix_within, d_c_scores, d_b_scores = lax.optimization_barrier(
            (got, within, d_x_within, d_prefix_within, d_c_scores, d_b_scores)
        )
        rows = scan_rows(got, head_count, HEADDIM, count, split)
        incoming, adjoint = send_back(rows, head_count, HEADDIM, count)
    else:
        incoming = jnp.zeros_like(local)
        adjoint = jnp.zeros_like(local)

    starts = [incoming]
    for k in range(blocks - 1):
        starts.append(gain[:, k, None, None] * starts[-1] + states[:, k])
    start = jnp.stack(starts, axis=1)
    carried = split_dot("ktn,hkpn->hktp", c16, start)
    out = within + e_prefix[..., None] * carried
    outputs = out.transpose(1, 2, 0, 3).reshape(tokens, head_count * HEADDIM).astype(BF16)

    d_prefix = jnp.sum(g_scaled * carried, axis=-1) + d_prefix_within
    d_c = jnp.einsum("hktp,hkpn->ktn", g_scaled, start, precision=lax.Precision.HIGH) + d_c_scores

    lam = adjoint
    d_states = [None] * blocks
    d_totals = [None] * blocks
    for k in reversed(range(blocks)):
        d_states[k] = lam
        d_totals[k] = gain[:, k] * jnp.sum(lam * start[:, k], axis=(1, 2))
        lam = start_grad[:, k] + gain[:, k, None, None] * lam
    d_states = jnp.stack(d_states, axis=1)
    d_totals = jnp.stack(d_totals, axis=1)

    d_scaled = rounded(split_dot("ksn,hkpn->hksp", b16, d_states))
    d_b = split_dot("hksp,hkpn->ksn", scaled, d_states) + d_b_scores
    d_x = d_scaled * last_w[..., None] + d_x_within
    d_last = jnp.sum(d_scaled * xf, axis=-1) * last_w
    d_prefix = d_prefix - d_last
    d_totals = d_totals + jnp.sum(d_last, axis=-1)

    d_prefix = d_prefix.at[..., -1].add(d_totals)
    d_decay = lax.cumsum(d_prefix, axis=2, reverse=True)
    grad_decay = d_decay.transpose(1, 2, 0).reshape(tokens, head_count)
    grad_inputs = d_x.transpose(1, 2, 0, 3).reshape(tokens, head_count * HEADDIM).astype(BF16)
    grad_b, grad_c = head_sum((d_b.reshape(tokens, STATE), d_c.reshape(tokens, STATE)), head_size)
    return (outputs, grad_inputs, grad_decay, grad_b, grad_c)


def solution(mesh):
    seq_size = mesh.shape["seq"]
    head_size = mesh.shape["head"]
    split = 2 if seq_size % 4 == 0 else 1
    count = seq_size // split
    grid = Mesh(mesh.devices.reshape(split, count, head_size), ("hi", "lo", "head"))
    seq = ("hi", "lo")
    placed = (P(seq, "head"), P(seq, "head"), P(seq, None), P(seq, None), P(seq, "head"))

    def body(inputs, log_decay, b_proj, c_proj, grad_out):
        return shards(inputs, log_decay, b_proj, c_proj, grad_out, count, head_size, split)

    return jax.shard_map(
        body,
        mesh=grid,
        in_specs=placed,
        out_specs=(P(seq, "head"), P(seq, "head"), P(seq, "head"), P(seq, None), P(seq, None)),
        check_vma=False,
    )
```
